256 devices in a mesh: resp: 32 (over y, x, core), head: 8 (over z).
Axes of the slice: x: 4, y: 4, z: 8, core: 2. Of those that a mesh axis runs over, the one named last changes fastest.
Arguments:
- queries: bfloat16 [32, 512, 8192], P('resp', None, 'head'), may hold values from -18 to 18
- key_states: bfloat16 [32, 512, 1024], P('resp', None, 'head'), may hold values from -6 to 6
- value_states: bfloat16 [32, 512, 1024], P('resp', None, 'head'), may hold values from -30 to 30
- partners: int32 [32, 3], P('resp'), may hold values from 0 to 31, as said below
- counts: int32 [32], P('resp'), may hold values from 1 to 3, as said below
- norm_gain: float32 [8192], P('head'), may hold values from 0.25 to 1.75
- out_grad: bfloat16 [32, 512, 8192], P('resp', None, 'head'), may hold values from -6 to 6
Outputs:
- normed_out: bfloat16 [32, 512, 8192], P('resp', None, 'head')
- query_grads: bfloat16 [32, 512, 8192], P('resp', None, 'head')
- key_grads: bfloat16 [32, 512, 1024], P('resp', None, 'head')
- value_grads: bfloat16 [32, 512, 1024], P('resp', None, 'head')
The draws below stay inside these ranges and needn't reach their ends.
Inputs may be any that keep to these rules, and one draw needn't show every extreme that they name: Row r lists 3 different partners, all in the aligned block of 8 responses that holds r, none equal to r; the first counts[r] of them are live, the rest unused. Live partnership is symmetric: b is a live partner of a exactly when a is a live partner of b. `counts`: some response has 3 live partners.
All inputs are finite; a program needn't handle non-finite values.
Results may differ from the reference program's by a relative error of at most 0.015.
Values may be sent and summed in bfloat16 or wider, within the bound.
No kernel may reach another device: no remote copies, remote signals or barrier semaphores. Data moves between devices by JAX's collectives and lax.ppermute only.
A program may use at most 64 MiB of HBM per device.

```python
import jax
import jax.numpy as jnp
from jax import lax

QHEADS = 64
KVHEADS = 8
HD = 128
D = 8192
L = 512
GROUP = 8
SLOTS = 3
RESPONSES = 32


def pair_table(key):
    base = jax.random.fold_in(key, 5)
    group_count = RESPONSES // GROUP
    cluster_key_rows = jax.random.split(jax.random.fold_in(base, 1), group_count)
    masks = jax.vmap(lambda single: jax.random.permutation(single, GROUP - 1) + 1)(cluster_key_rows)[:, :SLOTS]
    masks = masks.astype(jnp.int32)
    response = jnp.arange(RESPONSES, dtype=jnp.int32)
    place = response % GROUP
    first = response - place
    row_masks = masks[response // GROUP]
    partner = first[:, None] + jnp.bitwise_xor(place[:, None], row_masks)
    coin = jax.random.randint(jax.random.fold_in(base, 2), (RESPONSES, SLOTS), 0, 2).astype(jnp.int32)
    slot_grid = jnp.broadcast_to(jnp.arange(SLOTS, dtype=jnp.int32)[None, :], (RESPONSES, SLOTS))
    lower = jnp.minimum(response[:, None], partner)
    pair_coin = coin[lower, slot_grid]
    live = (pair_coin == 1) | (slot_grid == 0) | (response[:, None] == 0) | (partner == 0)
    order_key = (1 - live.astype(jnp.int32)) * SLOTS + slot_grid
    order = jnp.argsort(order_key, axis=1)
    sorted_partner = jnp.take_along_axis(partner, order, axis=1).astype(jnp.int32)
    live_counts = jnp.sum(live.astype(jnp.int32), axis=1).astype(jnp.int32)
    return (sorted_partner, live_counts)


def draw_partners(key, part):
    return pair_table(key)[0]


def draw_counts(key, part):
    return pair_table(key)[1]


def draw_queries(key, part):
    base = jnp.clip(jax.random.normal(jax.random.fold_in(key, 31), (RESPONSES, L, QHEADS, HD), jnp.float32), -6.0, 6.0)
    return base.reshape(RESPONSES, L, D).astype(jnp.bfloat16)


def draw_key_states(key, part):
    base = jnp.clip(jax.random.normal(jax.random.fold_in(key, 41), (RESPONSES, L, KVHEADS, HD), jnp.float32), -6.0, 6.0)
    return base.reshape(RESPONSES, L, KVHEADS * HD).astype(jnp.bfloat16)


def draw_value_states(key, part):
    base = jnp.clip(jax.random.normal(jax.random.fold_in(key, 51), (RESPONSES, L, KVHEADS, HD), jnp.float32), -6.0, 6.0)
    head_pos = jnp.arange(KVHEADS, dtype=jnp.float32) / (KVHEADS - 1)
    spread = jnp.exp(jax.random.uniform(jax.random.fold_in(key, 52), (KVHEADS,), jnp.float32, -0.25, 0.25))
    head_scale = 0.6 * 3.0 ** head_pos * spread
    base = base * head_scale[None, None, :, None]
    return base.reshape(RESPONSES, L, KVHEADS * HD).astype(jnp.bfloat16)


def block_scale(stream_key, dims, cuts, smallest, top_value):
    gain = 1.0
    for axis_at, shards_of in cuts:
        draws = jax.random.uniform(jax.random.fold_in(jax.random.fold_in(stream_key, 6), axis_at), (shards_of,), jnp.float32, smallest / len(cuts), top_value / len(cuts))
        gain = gain * jnp.repeat(jnp.exp(draws), dims[axis_at] // shards_of).reshape((-1,) + (1,) * (len(dims) - 1 - axis_at))
    return gain


def centred(own_key, extent, width, bound, pieces=(), held_as=jnp.bfloat16):
    entries = jax.random.normal(own_key, extent, jnp.float32) * width
    if len(pieces) > 0:
        entries = block_scale(own_key, extent, pieces, -0.22, 0.18) * entries
    return jnp.clip(entries, min=-bound, max=bound).astype(held_as)


def setup_inputs(seed: int = 0) -> dict:
    keys = jax.random.split(jax.random.key(seed), 8)
    queries = draw_queries(jax.random.fold_in(keys[7], 71), 0)
    key_states = draw_key_states(jax.random.fold_in(keys[7], 71), 0)
    value_states = draw_value_states(jax.random.fold_in(keys[7], 71), 0)
    partners = draw_partners(jax.random.fold_in(keys[7], 71), 0)
    counts = draw_counts(jax.random.fold_in(keys[7], 71), 0)
    norm_gain = jnp.clip(1.0 + 0.15 * jax.random.normal(keys[5], (D,), jnp.float32), 0.25, 1.75)
    out_grad = centred(keys[6], (RESPONSES, L, D), 1.0, 6.0, ((0, 32), (2, 8)))
    return {"queries": queries, "key_states": key_states, "value_states": value_states, "partners": partners, "counts": counts, "norm_gain": norm_gain, "out_grad": out_grad}


EPSILON = 1e-05
NEG_FLOOR = -1e+30

def head_forward(query_head, mate_keys, mate_values, live_mask):
    scores = jnp.einsum('qgd,jkd->qgjk', query_head, mate_keys, precision=lax.Precision.HIGHEST) * HD ** (-0.5)
    masked = jnp.where(live_mask[None, None, :, None], scores, NEG_FLOOR)
    row_max = lax.optimization_barrier(jnp.max(masked, axis=(2, 3)))
    exps = jnp.exp(masked - row_max[:, :, None, None])
    denominator = lax.optimization_barrier(jnp.sum(exps, axis=(2, 3)))
    rounded = lax.optimization_barrier(exps.astype(jnp.bfloat16)).astype(jnp.float32)
    weighted = jnp.einsum('qgjk,jkd->qgd', rounded, mate_values, precision=lax.Precision.HIGHEST)
    attention = (weighted / denominator[:, :, None]).astype(jnp.bfloat16)
    return (attention, row_max + jnp.log(denominator))

def head_backward(query_head, mate_keys, mate_values, grad_head, attention_head, log_total, live_mask):
    score_scale = HD ** (-0.5)
    row_delta = lax.optimization_barrier(jnp.sum(grad_head * attention_head.astype(jnp.float32), -1))
    scores = jnp.einsum('qgd,jkd->qgjk', query_head, mate_keys, precision=lax.Precision.HIGHEST) * score_scale
    masked = jnp.where(live_mask[None, None, :, None], scores, NEG_FLOOR)
    back_probs = jnp.exp(masked - log_total[:, :, None, None])
    rounded = lax.optimization_barrier(back_probs.astype(jnp.bfloat16)).astype(jnp.float32)
    value_term = jnp.einsum('qgjk,qgd->jkd', rounded, grad_head, precision=lax.Precision.HIGHEST)
    prob_grad = jnp.einsum('qgd,jkd->qgjk', grad_head, mate_values, precision=lax.Precision.HIGHEST)
    score_grad = back_probs * (prob_grad - row_delta[:, :, None, None])
    score_grad = lax.optimization_barrier(score_grad.astype(jnp.bfloat16)).astype(jnp.float32)
    query_grad = score_scale * jnp.einsum('qgjk,jkd->qgd', score_grad, mate_keys, precision=lax.Precision.HIGHEST)
    key_term = score_scale * jnp.einsum('qgjk,qgd->jkd', score_grad, query_head, precision=lax.Precision.HIGHEST)
    return (query_grad, key_term, value_term)

def reference(queries, key_states, value_states, partners, counts, norm_gain, out_grad):
    per_group = QHEADS // KVHEADS
    slot_numbers = jnp.arange(SLOTS, dtype=jnp.int32)
    gain_float = norm_gain.astype(jnp.float32)

    def one_response(running, response):
        key_total, value_total = running
        mate_ids = partners[response].astype(jnp.int32)
        live_mask = slot_numbers < counts[response]
        query_heads = jnp.moveaxis(queries[response].astype(jnp.float32).reshape(L, KVHEADS, per_group, HD), 1, 0)
        mate_keys = jnp.moveaxis(key_states[mate_ids].astype(jnp.float32).reshape(SLOTS, L, KVHEADS, HD), 2, 0)
        mate_values = jnp.moveaxis(value_states[mate_ids].astype(jnp.float32).reshape(SLOTS, L, KVHEADS, HD), 2, 0)
        attention_heads, log_total = lax.map(lambda parts: head_forward(parts[0], parts[1], parts[2], live_mask), (query_heads, mate_keys, mate_values))
        attention = jnp.moveaxis(attention_heads, 0, 1).reshape(L, D).astype(jnp.float32)
        inverse_rms = lax.rsqrt(lax.optimization_barrier(jnp.mean(attention * attention, -1)) + EPSILON)
        normed = (attention * inverse_rms[:, None] * gain_float).astype(jnp.bfloat16)
        scaled_grad = out_grad[response].astype(jnp.float32) * gain_float
        dot_sums = lax.optimization_barrier(jnp.sum(attention * scaled_grad, -1))
        attention_grad = inverse_rms[:, None] * scaled_grad - attention * (inverse_rms ** 3 * dot_sums / D)[:, None]
        attention_grad = attention_grad.astype(jnp.bfloat16)
        grad_heads = jnp.moveaxis(attention_grad.astype(jnp.float32).reshape(L, KVHEADS, per_group, HD), 1, 0)
        query_grad, key_term, value_term = lax.map(lambda parts: head_backward(parts[0], parts[1], parts[2], parts[3], parts[4], parts[5], live_mask), (query_heads, mate_keys, mate_values, grad_heads, attention_heads, log_total))
        query_out = jnp.moveaxis(query_grad, 0, 1).reshape(L, D).astype(jnp.bfloat16)
        key_term = jnp.moveaxis(key_term, 0, 2).reshape(SLOTS, L, KVHEADS * HD)
        value_term = jnp.moveaxis(value_term, 0, 2).reshape(SLOTS, L, KVHEADS * HD)
        key_total = key_total.at[mate_ids].add(key_term)
        value_total = value_total.at[mate_ids].add(value_term)
        return ((key_total, value_total), (normed, query_out))
    zero_total = jnp.zeros((RESPONSES, L, KVHEADS * HD), jnp.float32)
    totals, outputs = lax.scan(one_response, (zero_total, zero_total), jnp.arange(RESPONSES, dtype=jnp.int32))
    return (outputs[0], outputs[1], totals[0].astype(jnp.bfloat16), totals[1].astype(jnp.bfloat16))
```

```python
import jax
import jax.numpy as jnp
from jax import lax
from jax.sharding import PartitionSpec as P

HD = 128
D = 8192
GROUP = 8


EPSILON = 1e-05
NEG_FLOOR = -1e30


def add_row(buffer, addend, row_index):
    current = lax.dynamic_index_in_dim(buffer, row_index, 0, keepdims=False)
    return lax.dynamic_update_index_in_dim(buffer, current + addend, row_index, 0)


def body(queries, key_states, value_states, partners, counts, norm_gain, out_grad):
    my_index = lax.axis_index("resp")
    seq_len = queries.shape[1]
    kv_cols = key_states.shape[2]
    kv_heads = kv_cols // HD
    per_group = queries.shape[2] // kv_cols
    resp_count = lax.axis_size("resp")

    def by_distance(block):
        rows = [block]
        for distance in range(1, GROUP):
            route = [(low, low ^ distance) for low in range(resp_count)]
            rows.append(lax.ppermute(block, "resp", route))
        return jnp.concatenate(rows, 0)

    cluster_key_rows = by_distance(key_states)
    group_values = by_distance(value_states)
    query_heads = queries[0].reshape(seq_len, kv_heads, per_group, HD)
    score_scale = HD ** (-0.5)
    mate_rows = jnp.bitwise_xor(partners[0], my_index)
    live_count = counts[0]

    def partner_block_tile(slot_index):
        mate_row = mate_rows[slot_index]
        mate_keys = lax.dynamic_index_in_dim(cluster_key_rows, mate_row, 0, keepdims=False).reshape(
            seq_len, kv_heads, HD
        )
        mate_values = lax.dynamic_index_in_dim(group_values, mate_row, 0, keepdims=False).reshape(
            seq_len, kv_heads, HD
        )
        return (mate_keys, mate_values)

    def score_block(mate_keys):
        return (
            jnp.einsum("qhgd,khd->qhgk", query_heads, mate_keys, preferred_element_type=jnp.float32)
            * score_scale
        )

    def forward_step(slot_index, running):
        running_max, denominator, weighted = running
        mate_keys, mate_values = partner_block_tile(slot_index)
        scores = score_block(mate_keys)
        new_max = jnp.maximum(running_max, jnp.max(scores, -1))
        rescale = jnp.exp(running_max - new_max)
        weights = jnp.exp(scores - new_max[..., None])
        denominator = denominator * rescale + jnp.sum(weights, -1)
        weighted = weighted * rescale[..., None] + jnp.einsum(
            "qhgk,khd->qhgd",
            weights.astype(jnp.bfloat16),
            mate_values,
            preferred_element_type=jnp.float32,
        )
        return (new_max, denominator, weighted)

    stat_shape = (seq_len, kv_heads, per_group)
    start_state = (
        jnp.full(stat_shape, NEG_FLOOR, jnp.float32),
        jnp.zeros(stat_shape, jnp.float32),
        jnp.zeros(stat_shape + (HD,), jnp.float32),
    )
    running_max, denominator, weighted = lax.fori_loop(0, live_count, forward_step, start_state)
    attention = (weighted / denominator[..., None]).astype(jnp.bfloat16)
    log_total = running_max + jnp.log(denominator)
    attention_flat = attention.reshape(seq_len, -1).astype(jnp.float32)
    square_sums = lax.psum(jnp.sum(attention_flat * attention_flat, -1), "head")
    inverse_rms = lax.rsqrt(square_sums / D + EPSILON)
    normed_out = (attention_flat * inverse_rms[:, None] * norm_gain).astype(jnp.bfloat16)[None]
    scaled_grad = out_grad[0].astype(jnp.float32) * norm_gain
    dot_sums = lax.psum(jnp.sum(attention_flat * scaled_grad, -1), "head")
    attention_grad = (
        inverse_rms[:, None] * scaled_grad
        - attention_flat * (inverse_rms**3 * dot_sums / D)[:, None]
    )
    attention_grad = attention_grad.astype(jnp.bfloat16).reshape(seq_len, kv_heads, per_group, HD)
    row_delta = jnp.sum(attention_grad.astype(jnp.float32) * attention.astype(jnp.float32), -1)

    def backward_step(slot_index, running):
        query_grad, key_buffer, value_storage = running
        mate_keys, mate_values = partner_block_tile(slot_index)
        back_probs = jnp.exp(score_block(mate_keys) - log_total[..., None])
        value_term = jnp.einsum(
            "qhgk,qhgd->khd",
            back_probs.astype(jnp.bfloat16),
            attention_grad,
            preferred_element_type=jnp.float32,
        )
        prob_grad = jnp.einsum(
            "qhgd,khd->qhgk", attention_grad, mate_values, preferred_element_type=jnp.float32
        )
        score_grad = (back_probs * (prob_grad - row_delta[..., None])).astype(jnp.bfloat16)
        query_grad = query_grad + score_scale * jnp.einsum(
            "qhgk,khd->qhgd", score_grad, mate_keys, preferred_element_type=jnp.float32
        )
        key_term = score_scale * jnp.einsum(
            "qhgk,qhgd->khd", score_grad, query_heads, preferred_element_type=jnp.float32
        )
        mate_row = mate_rows[slot_index]
        key_buffer = add_row(key_buffer, key_term.reshape(seq_len, kv_cols), mate_row)
        value_storage = add_row(value_storage, value_term.reshape(seq_len, kv_cols), mate_row)
        return (query_grad, key_buffer, value_storage)

    zero_buffer = jnp.zeros((GROUP, seq_len, kv_cols), jnp.float32)
    query_grad, key_buffer, value_storage = lax.fori_loop(
        0,
        live_count,
        backward_step,
        (jnp.zeros(stat_shape + (HD,), jnp.float32), zero_buffer, zero_buffer),
    )
    query_grads = query_grad.reshape(seq_len, -1).astype(jnp.bfloat16)[None]
    def to_owners(buffer):
        total = jnp.zeros(buffer.shape[1:], jnp.float32)
        for distance in range(1, GROUP):
            route = [(low, low ^ distance) for low in range(resp_count)]
            sent = buffer[distance].astype(jnp.bfloat16)
            total = total + lax.ppermute(sent, "resp", route).astype(jnp.float32)
        return total[None]

    key_total = to_owners(key_buffer)
    value_total = to_owners(value_storage)
    return (
        normed_out,
        query_grads,
        key_total.astype(jnp.bfloat16),
        value_total.astype(jnp.bfloat16),
    )


def solution(mesh):
    placed = (
        P("resp", None, "head"),
        P("resp", None, "head"),
        P("resp", None, "head"),
        P("resp", None),
        P("resp"),
        P("head"),
        P("resp", None, "head"),
    )
    return jax.shard_map(
        body,
        mesh=mesh,
        in_specs=placed,
        out_specs=(
            P("resp", None, "head"),
            P("resp", None, "head"),
            P("resp", None, "head"),
            P("resp", None, "head"),
        ),
        check_vma=False,
    )
```

```python
import jax
import jax.numpy as jnp
from jax import lax
from jax.sharding import PartitionSpec as P

HD = 128
D = 8192
GROUP = 8


EPSILON = 1e-05
NEG_FLOOR = -1e30


def add_row(buffer, addend, row_index):
    current = lax.dynamic_index_in_dim(buffer, row_index, 0, keepdims=False)
    return lax.dynamic_update_index_in_dim(buffer, current + addend, row_index, 0)


def head_sum(row_part):
    return jnp.sum(lax.all_gather(row_part, "head"), 0)


def body(queries, key_states, value_states, partners, counts, norm_gain, out_grad):
    seq_len = queries.shape[1]
    kv_cols = key_states.shape[2]
    kv_heads = kv_cols // HD
    per_group = queries.shape[2] // kv_cols
    group_size = lax.axis_size("grp")
    my_place = lax.axis_index("grp")
    both_states = jnp.concatenate([key_states[0], value_states[0]], -1)
    group_states = lax.all_gather(both_states, "grp")
    cluster_key_rows = group_states[..., :kv_cols]
    group_values = group_states[..., kv_cols:]
    query_heads = queries[0].reshape(seq_len, kv_heads, per_group, HD)
    score_scale = HD ** (-0.5)
    mate_rows = partners[0] % group_size
    live_count = counts[0]

    def partner_block_tile(slot_index):
        mate_row = mate_rows[slot_index]
        mate_keys = lax.dynamic_index_in_dim(cluster_key_rows, mate_row, 0, keepdims=False).reshape(
            seq_len, kv_heads, HD
        )
        mate_values = lax.dynamic_index_in_dim(group_values, mate_row, 0, keepdims=False).reshape(
            seq_len, kv_heads, HD
        )
        return (mate_keys, mate_values)

    def score_block(mate_keys):
        return (
            jnp.einsum("qhgd,khd->qhgk", query_heads, mate_keys, preferred_element_type=jnp.float32)
            * score_scale
        )

    def forward_step(slot_index, running):
        running_max, denominator, weighted = running
        mate_keys, mate_values = partner_block_tile(slot_index)
        scores = score_block(mate_keys)
        new_max = jnp.maximum(running_max, jnp.max(scores, -1))
        rescale = jnp.exp(running_max - new_max)
        weights = jnp.exp(scores - new_max[..., None])
        denominator = denominator * rescale + jnp.sum(weights, -1)
        weighted = weighted * rescale[..., None] + jnp.einsum(
            "qhgk,khd->qhgd",
            weights.astype(jnp.bfloat16),
            mate_values,
            preferred_element_type=jnp.float32,
        )
        return (new_max, denominator, weighted)

    stat_shape = (seq_len, kv_heads, per_group)
    start_state = (
        jnp.full(stat_shape, NEG_FLOOR, jnp.float32),
        jnp.zeros(stat_shape, jnp.float32),
        jnp.zeros(stat_shape + (HD,), jnp.float32),
    )
    running_max, denominator, weighted = lax.fori_loop(0, live_count, forward_step, start_state)
    attention = (weighted / denominator[..., None]).astype(jnp.bfloat16)
    log_total = running_max + jnp.log(denominator)
    attention_flat = attention.reshape(seq_len, -1).astype(jnp.float32)
    square_sums = head_sum(jnp.sum(attention_flat * attention_flat, -1))
    inverse_rms = lax.rsqrt(square_sums / D + EPSILON)
    normed_out = (attention_flat * inverse_rms[:, None] * norm_gain).astype(jnp.bfloat16)[None]
    scaled_grad = out_grad[0].astype(jnp.float32) * norm_gain
    dot_sums = head_sum(jnp.sum(attention_flat * scaled_grad, -1))
    attention_grad = (
        inverse_rms[:, None] * scaled_grad
        - attention_flat * (inverse_rms**3 * dot_sums / D)[:, None]
    )
    attention_grad = attention_grad.astype(jnp.bfloat16).reshape(seq_len, kv_heads, per_group, HD)
    row_delta = jnp.sum(attention_grad.astype(jnp.float32) * attention.astype(jnp.float32), -1)

    def backward_step(slot_index, running):
        query_grad, key_buffer, value_storage = running
        mate_keys, mate_values = partner_block_tile(slot_index)
        back_probs = jnp.exp(score_block(mate_keys) - log_total[..., None])
        value_term = jnp.einsum(
            "qhgk,qhgd->khd",
            back_probs.astype(jnp.bfloat16),
            attention_grad,
            preferred_element_type=jnp.float32,
        )
        prob_grad = jnp.einsum(
            "qhgd,khd->qhgk", attention_grad, mate_values, preferred_element_type=jnp.float32
        )
        score_grad = (back_probs * (prob_grad - row_delta[..., None])).astype(jnp.bfloat16)
        query_grad = query_grad + score_scale * jnp.einsum(
            "qhgk,khd->qhgd", score_grad, mate_keys, preferred_element_type=jnp.float32
        )
        key_term = score_scale * jnp.einsum(
            "qhgk,qhgd->khd", score_grad, query_heads, preferred_element_type=jnp.float32
        )
        mate_row = mate_rows[slot_index]
        key_buffer = add_row(key_buffer, key_term.reshape(seq_len, kv_cols), mate_row)
        value_storage = add_row(value_storage, value_term.reshape(seq_len, kv_cols), mate_row)
        return (query_grad, key_buffer, value_storage)

    zero_buffer = jnp.zeros((GROUP, seq_len, kv_cols), jnp.float32)
    query_grad, key_buffer, value_storage = lax.fori_loop(
        0,
        live_count,
        backward_step,
        (jnp.zeros(stat_shape + (HD,), jnp.float32), zero_buffer, zero_buffer),
    )
    query_grads = query_grad.reshape(seq_len, -1).astype(jnp.bfloat16)[None]
    both_terms = jnp.concatenate([key_buffer, value_storage], -1).astype(jnp.bfloat16)
    both_totals = lax.psum_scatter(both_terms, "grp", scatter_dimension=0, tiled=True)
    key_total = both_totals[..., :kv_cols]
    value_total = both_totals[..., kv_cols:]
    return (
        normed_out,
        query_grads,
        key_total.astype(jnp.bfloat16),
        value_total.astype(jnp.bfloat16),
    )


def solution(mesh):
    placed = (
        P("resp", None, "head"),
        P("resp", None, "head"),
        P("resp", None, "head"),
        P("resp", None),
        P("resp"),
        P("head"),
        P("resp", None, "head"),
    )
    group_count = mesh.shape["resp"] // GROUP
    grouped = jax.sharding.Mesh(
        mesh.devices.reshape(group_count, GROUP, mesh.shape["head"]), ("blk", "grp", "head")
    )
    placed = jax.tree.map(
        lambda spec: P(*[("blk", "grp") if name == "resp" else name for name in spec]), placed
    )
    return jax.shard_map(
        body,
        mesh=grouped,
        in_specs=placed,
        out_specs=(
            P(("blk", "grp"), None, "head"),
            P(("blk", "grp"), None, "head"),
            P(("blk", "grp"), None, "head"),
            P(("blk", "grp"), None, "head"),
        ),
        check_vma=False,
    )
```

```python
import jax
import jax.numpy as jnp
from jax import lax
from jax.sharding import PartitionSpec as P

HD = 128
D = 8192
GROUP = 8


EPSILON = 1e-05
NEG_FLOOR = -1e30


def add_row(buffer, addend, row_index):
    current = lax.dynamic_index_in_dim(buffer, row_index, 0, keepdims=False)
    return lax.dynamic_update_index_in_dim(buffer, current + addend, row_index, 0)


def body(queries, key_states, value_states, partners, counts, norm_gain, out_grad):
    my_index = lax.axis_index("resp")
    seq_len = queries.shape[1]
    kv_cols = key_states.shape[2]
    kv_heads = kv_cols // HD
    per_group = queries.shape[2] // kv_cols
    resp_count = lax.axis_size("resp")

    def exchange(block, axis, bit):
        route = [(low, low ^ (1 << bit)) for low in range(lax.axis_size(axis))]
        return lax.ppermute(block, axis, route)

    group_states = jnp.concatenate([key_states, value_states], -1)
    for bit in range(GROUP.bit_length() - 1):
        group_states = jnp.concatenate([group_states, exchange(group_states, "resp", bit)], 0)
    cluster_key_rows = group_states[..., :kv_cols]
    group_values = group_states[..., kv_cols:]
    query_heads = queries[0].reshape(seq_len, kv_heads, per_group, HD)
    score_scale = HD ** (-0.5)
    mate_rows = jnp.bitwise_xor(partners[0], my_index)
    live_count = counts[0]

    def partner_block_tile(slot_index):
        mate_row = mate_rows[slot_index]
        mate_keys = lax.dynamic_index_in_dim(cluster_key_rows, mate_row, 0, keepdims=False).reshape(
            seq_len, kv_heads, HD
        )
        mate_values = lax.dynamic_index_in_dim(group_values, mate_row, 0, keepdims=False).reshape(
            seq_len, kv_heads, HD
        )
        return (mate_keys, mate_values)

    def score_block(mate_keys):
        return (
            jnp.einsum("qhgd,khd->qhgk", query_heads, mate_keys, preferred_element_type=jnp.float32)
            * score_scale
        )

    def forward_step(slot_index, running):
        running_max, denominator, weighted = running
        mate_keys, mate_values = partner_block_tile(slot_index)
        scores = score_block(mate_keys)
        new_max = jnp.maximum(running_max, jnp.max(scores, -1))
        rescale = jnp.exp(running_max - new_max)
        weights = jnp.exp(scores - new_max[..., None])
        denominator = denominator * rescale + jnp.sum(weights, -1)
        weighted = weighted * rescale[..., None] + jnp.einsum(
            "qhgk,khd->qhgd",
            weights.astype(jnp.bfloat16),
            mate_values,
            preferred_element_type=jnp.float32,
        )
        return (new_max, denominator, weighted)

    stat_shape = (seq_len, kv_heads, per_group)
    start_state = (
        jnp.full(stat_shape, NEG_FLOOR, jnp.float32),
        jnp.zeros(stat_shape, jnp.float32),
        jnp.zeros(stat_shape + (HD,), jnp.float32),
    )
    running_max, denominator, weighted = lax.fori_loop(0, live_count, forward_step, start_state)
    attention = (weighted / denominator[..., None]).astype(jnp.bfloat16)
    log_total = running_max + jnp.log(denominator)
    attention_flat = attention.reshape(seq_len, -1).astype(jnp.float32)
    scaled_grad = out_grad[0].astype(jnp.float32) * norm_gain
    row_sums = jnp.stack(
        [jnp.sum(attention_flat * attention_flat, -1), jnp.sum(attention_flat * scaled_grad, -1)]
    )
    for bit in range(lax.axis_size("head").bit_length() - 1):
        row_sums = row_sums + exchange(row_sums, "head", bit)
    square_sums, dot_sums = row_sums[0], row_sums[1]
    inverse_rms = lax.rsqrt(square_sums / D + EPSILON)
    normed_out = (attention_flat * inverse_rms[:, None] * norm_gain).astype(jnp.bfloat16)[None]
    attention_grad = (
        inverse_rms[:, None] * scaled_grad
        - attention_flat * (inverse_rms**3 * dot_sums / D)[:, None]
    )
    attention_grad = attention_grad.astype(jnp.bfloat16).reshape(seq_len, kv_heads, per_group, HD)
    row_delta = jnp.sum(attention_grad.astype(jnp.float32) * attention.astype(jnp.float32), -1)

    def backward_step(slot_index, running):
        query_grad, key_buffer, value_storage = running
        mate_keys, mate_values = partner_block_tile(slot_index)
        back_probs = jnp.exp(score_block(mate_keys) - log_total[..., None])
        value_term = jnp.einsum(
            "qhgk,qhgd->khd",
            back_probs.astype(jnp.bfloat16),
            attention_grad,
            preferred_element_type=jnp.float32,
        )
        prob_grad = jnp.einsum(
            "qhgd,khd->qhgk", attention_grad, mate_values, preferred_element_type=jnp.float32
        )
        score_grad = (back_probs * (prob_grad - row_delta[..., None])).astype(jnp.bfloat16)
        query_grad = query_grad + score_scale * jnp.einsum(
            "qhgk,khd->qhgd", score_grad, mate_keys, preferred_element_type=jnp.float32
        )
        key_term = score_scale * jnp.einsum(
            "qhgk,qhgd->khd", score_grad, query_heads, preferred_element_type=jnp.float32
        )
        mate_row = mate_rows[slot_index]
        key_buffer = add_row(key_buffer, key_term.reshape(seq_len, kv_cols), mate_row)
        value_storage = add_row(value_storage, value_term.reshape(seq_len, kv_cols), mate_row)
        return (query_grad, key_buffer, value_storage)

    zero_buffer = jnp.zeros((GROUP, seq_len, kv_cols), jnp.float32)
    query_grad, key_buffer, value_storage = lax.fori_loop(
        0,
        live_count,
        backward_step,
        (jnp.zeros(stat_shape + (HD,), jnp.float32), zero_buffer, zero_buffer),
    )
    query_grads = query_grad.reshape(seq_len, -1).astype(jnp.bfloat16)[None]
    both_terms = jnp.concatenate([key_buffer, value_storage], -1)
    for bit in reversed(range(GROUP.bit_length() - 1)):
        half = 1 << bit
        sent = both_terms[half : 2 * half].astype(jnp.bfloat16)
        both_terms = both_terms[:half] + exchange(sent, "resp", bit).astype(jnp.float32)
    key_total = both_terms[..., :kv_cols]
    value_total = both_terms[..., kv_cols:]
    return (
        normed_out,
        query_grads,
        key_total.astype(jnp.bfloat16),
        value_total.astype(jnp.bfloat16),
    )


def solution(mesh):
    placed = (
        P("resp", None, "head"),
        P("resp", None, "head"),
        P("resp", None, "head"),
        P("resp", None),
        P("resp"),
        P("head"),
        P("resp", None, "head"),
    )
    return jax.shard_map(
        body,
        mesh=mesh,
        in_specs=placed,
        out_specs=(
            P("resp", None, "head"),
            P("resp", None, "head"),
            P("resp", None, "head"),
            P("resp", None, "head"),
        ),
        check_vma=False,
    )
```

```python
import functools

import jax
import jax.numpy as jnp
from jax import lax
from jax.experimental import pallas as pl
from jax.experimental.pallas import tpu as pltpu
from jax.sharding import PartitionSpec as P

HD = 128
D = 8192
GROUP = 8
SLOTS = 3


EPSILON = 1e-05
NEG_FLOOR = -1e30
SCORE_SCALE = HD ** (-0.5)

TRANS_B = (((1,), (1,)), ((), ()))
TRANS_A = (((0,), (0,)), ((), ()))


def slot_scores(count_ref, query_head, mate_keys, slot):
    scores = lax.dot_general(query_head, mate_keys, TRANS_B, preferred_element_type=jnp.float32)
    return jnp.where(slot < count_ref[0], scores * SCORE_SCALE, NEG_FLOOR)


def forward_kernel(count_ref, q_ref, k_ref, v_ref, out_ref, lse_ref):
    query_head = q_ref[...]
    scores = [slot_scores(count_ref, query_head, k_ref[slot], slot) for slot in range(SLOTS)]
    row_max = functools.reduce(
        jnp.maximum, [jnp.max(block, axis=1, keepdims=True) for block in scores]
    )
    exps = [jnp.exp(block - row_max) for block in scores]
    denominator = sum(jnp.sum(block, axis=1, keepdims=True) for block in exps)
    weighted = sum(
        jnp.dot(exps[slot].astype(jnp.bfloat16), v_ref[slot], preferred_element_type=jnp.float32)
        for slot in range(SLOTS)
    )
    out_ref[...] = (weighted / denominator).astype(out_ref.dtype)
    lse_ref[...] = jnp.broadcast_to(row_max + jnp.log(denominator), lse_ref.shape)


def backward_kernel(
    count_ref, q_ref, k_ref, v_ref, grad_ref, att_ref, lse_ref, dq_ref, dk_ref, dv_ref
):
    @pl.when(pl.program_id(0) == 0)
    def _():
        dk_ref[...] = jnp.zeros_like(dk_ref)
        dv_ref[...] = jnp.zeros_like(dv_ref)

    query_head = q_ref[...]
    grad_head = grad_ref[...]
    row_delta = jnp.sum(
        grad_head.astype(jnp.float32) * att_ref[...].astype(jnp.float32), axis=1, keepdims=True
    )
    log_total = lse_ref[:, :1]
    query_grad = jnp.zeros(dq_ref.shape, jnp.float32)
    for slot in range(SLOTS):
        mate_keys = k_ref[slot]
        back_probs = jnp.exp(slot_scores(count_ref, query_head, mate_keys, slot) - log_total)
        dv_ref[slot] += lax.dot_general(
            back_probs.astype(jnp.bfloat16), grad_head, TRANS_A, preferred_element_type=jnp.float32
        )
        prob_grad = lax.dot_general(
            grad_head, v_ref[slot], TRANS_B, preferred_element_type=jnp.float32
        )
        score_grad = (back_probs * (prob_grad - row_delta)).astype(jnp.bfloat16)
        query_grad = query_grad + jnp.dot(score_grad, mate_keys, preferred_element_type=jnp.float32)
        dk_ref[slot] += SCORE_SCALE * lax.dot_general(
            score_grad, query_head, TRANS_A, preferred_element_type=jnp.float32
        )
    dq_ref[...] = (SCORE_SCALE * query_grad).astype(dq_ref.dtype)


def attention_forward(count, queries, mate_keys, mate_values):
    seq_len, width = queries.shape
    heads = width // HD
    head_block = pl.BlockSpec((seq_len, HD), lambda h, c: (0, h))
    slot_block = pl.BlockSpec((SLOTS, seq_len, HD), lambda h, c: (0, 0, 0))
    return pl.pallas_call(
        forward_kernel,
        grid_spec=pltpu.PrefetchScalarGridSpec(
            num_scalar_prefetch=1,
            grid=(heads,),
            in_specs=[head_block, slot_block, slot_block],
            out_specs=[head_block, head_block],
        ),
        out_shape=[
            jax.ShapeDtypeStruct((seq_len, width), jnp.bfloat16),
            jax.ShapeDtypeStruct((seq_len, width), jnp.float32),
        ],
    )(count, queries, mate_keys, mate_values)


def attention_backward(count, queries, mate_keys, mate_values, attention_grad, attention, log_total):
    seq_len, width = queries.shape
    heads = width // HD
    head_block = pl.BlockSpec((seq_len, HD), lambda h, c: (0, h))
    slot_block = pl.BlockSpec((SLOTS, seq_len, HD), lambda h, c: (0, 0, 0))
    return pl.pallas_call(
        backward_kernel,
        grid_spec=pltpu.PrefetchScalarGridSpec(
            num_scalar_prefetch=1,
            grid=(heads,),
            in_specs=[head_block, slot_block, slot_block, head_block, head_block, head_block],
            out_specs=[head_block, slot_block, slot_block],
        ),
        out_shape=[
            jax.ShapeDtypeStruct((seq_len, width), jnp.bfloat16),
            jax.ShapeDtypeStruct((SLOTS, seq_len, HD), jnp.float32),
            jax.ShapeDtypeStruct((SLOTS, seq_len, HD), jnp.float32),
        ],
        compiler_params=pltpu.CompilerParams(dimension_semantics=("arbitrary",)),
    )(count, queries, mate_keys, mate_values, attention_grad, attention, log_total)


def exchange(block, axis, bit):
    route = [(low, low ^ (1 << bit)) for low in range(lax.axis_size(axis))]
    return lax.ppermute(block, axis, route)


def gather_group(block):
    for bit in range(GROUP.bit_length() - 1):
        block = jnp.concatenate([block, exchange(block, "resp", bit)], 0)
    return block


def return_group(terms):
    for bit in reversed(range(GROUP.bit_length() - 1)):
        half = 1 << bit
        sent = terms[half : 2 * half].astype(jnp.bfloat16)
        terms = terms[:half] + exchange(sent, "resp", bit).astype(jnp.float32)
    return terms


def body(queries, key_states, value_states, partners, counts, norm_gain, out_grad):
    my_index = lax.axis_index("resp")
    seq_len = queries.shape[1]
    mate_rows = jnp.bitwise_xor(partners[0], my_index)
    count = counts.astype(jnp.int32)
    mate_keys = jnp.take(gather_group(key_states), mate_rows, axis=0)
    mate_values = jnp.take(gather_group(value_states), mate_rows, axis=0)

    attention, log_total = attention_forward(count, queries[0], mate_keys, mate_values)
    attention_flat = attention.astype(jnp.float32)
    scaled_grad = out_grad[0].astype(jnp.float32) * norm_gain
    row_sums = jnp.stack(
        [jnp.sum(attention_flat * attention_flat, -1), jnp.sum(attention_flat * scaled_grad, -1)]
    )
    for bit in range(lax.axis_size("head").bit_length() - 1):
        row_sums = row_sums + exchange(row_sums, "head", bit)
    square_sums, dot_sums = row_sums[0], row_sums[1]
    inverse_rms = lax.rsqrt(square_sums / D + EPSILON)
    normed_out = (attention_flat * inverse_rms[:, None] * norm_gain).astype(jnp.bfloat16)[None]
    attention_grad = (
        inverse_rms[:, None] * scaled_grad
        - attention_flat * (inverse_rms**3 * dot_sums / D)[:, None]
    ).astype(jnp.bfloat16)

    query_grads, key_terms, value_terms = attention_backward(
        count, queries[0], mate_keys, mate_values, attention_grad, attention, log_total
    )
    zero_rows = jnp.zeros((GROUP,) + key_terms.shape[1:], jnp.float32)
    key_total = return_group(zero_rows.at[mate_rows].add(key_terms))
    value_total = return_group(zero_rows.at[mate_rows].add(value_terms))
    return (
        normed_out,
        query_grads[None],
        key_total.astype(jnp.bfloat16),
        value_total.astype(jnp.bfloat16),
    )


def solution(mesh):
    placed = (
        P("resp", None, "head"),
        P("resp", None, "head"),
        P("resp", None, "head"),
        P("resp", None),
        P("resp"),
        P("head"),
        P("resp", None, "head"),
    )
    return jax.shard_map(
        body,
        mesh=mesh,
        in_specs=placed,
        out_specs=(
            P("resp", None, "head"),
            P("resp", None, "head"),
            P("resp", None, "head"),
            P("resp", None, "head"),
        ),
        check_vma=False,
    )
```

```python
import functools

import jax
import jax.numpy as jnp
from jax import lax
from jax.experimental import pallas as pl
from jax.experimental.pallas import tpu as pltpu
from jax.sharding import PartitionSpec as P

HD = 128
D = 8192
GROUP = 8
SLOTS = 3


EPSILON = 1e-05
NEG_FLOOR = -1e30
SCORE_SCALE = HD ** (-0.5)

TRANS_B = (((1,), (1,)), ((), ()))
TRANS_A = (((0,), (0,)), ((), ()))


def slot_scores(count_ref, query_head, mate_keys, slot):
    scores = lax.dot_general(query_head, mate_keys, TRANS_B, preferred_element_type=jnp.float32)
    return jnp.where(slot < count_ref[0], scores * SCORE_SCALE, NEG_FLOOR)


def forward_kernel(count_ref, q_ref, k_ref, v_ref, out_ref, lse_ref):
    query_head = q_ref[...]
    scores = [slot_scores(count_ref, query_head, k_ref[slot], slot) for slot in range(SLOTS)]
    row_max = functools.reduce(
        jnp.maximum, [jnp.max(block, axis=1, keepdims=True) for block in scores]
    )
    exps = [jnp.exp(block - row_max) for block in scores]
    denominator = sum(jnp.sum(block, axis=1, keepdims=True) for block in exps)
    weighted = sum(
        jnp.dot(exps[slot].astype(jnp.bfloat16), v_ref[slot], preferred_element_type=jnp.float32)
        for slot in range(SLOTS)
    )
    out_ref[...] = (weighted / denominator).astype(out_ref.dtype)
    lse_ref[...] = jnp.broadcast_to(row_max + jnp.log(denominator), lse_ref.shape)


def backward_kernel(
    count_ref, q_ref, k_ref, v_ref, grad_ref, att_ref, lse_ref, dq_ref, dk_ref, dv_ref
):
    @pl.when(pl.program_id(0) == 0)
    def _():
        dk_ref[...] = jnp.zeros_like(dk_ref)
        dv_ref[...] = jnp.zeros_like(dv_ref)

    query_head = q_ref[...]
    grad_head = grad_ref[...]
    row_delta = jnp.sum(
        grad_head.astype(jnp.float32) * att_ref[...].astype(jnp.float32), axis=1, keepdims=True
    )
    log_total = lse_ref[:, :1]
    query_grad = jnp.zeros(dq_ref.shape, jnp.float32)
    for slot in range(SLOTS):
        mate_keys = k_ref[slot]
        back_probs = jnp.exp(slot_scores(count_ref, query_head, mate_keys, slot) - log_total)
        dv_ref[slot] += lax.dot_general(
            back_probs.astype(jnp.bfloat16), grad_head, TRANS_A, preferred_element_type=jnp.float32
        )
        prob_grad = lax.dot_general(
            grad_head, v_ref[slot], TRANS_B, preferred_element_type=jnp.float32
        )
        score_grad = (back_probs * (prob_grad - row_delta)).astype(jnp.bfloat16)
        query_grad = query_grad + jnp.dot(score_grad, mate_keys, preferred_element_type=jnp.float32)
        dk_ref[slot] += SCORE_SCALE * lax.dot_general(
            score_grad, query_head, TRANS_A, preferred_element_type=jnp.float32
        )
    dq_ref[...] = (SCORE_SCALE * query_grad).astype(dq_ref.dtype)


def attention_forward(count, queries, mate_keys, mate_values):
    seq_len, width = queries.shape
    heads = width // HD
    head_block = pl.BlockSpec((seq_len, HD), lambda h, c: (0, h))
    slot_block = pl.BlockSpec((SLOTS, seq_len, HD), lambda h, c: (0, 0, 0))
    return pl.pallas_call(
        forward_kernel,
        grid_spec=pltpu.PrefetchScalarGridSpec(
            num_scalar_prefetch=1,
            grid=(heads,),
            in_specs=[head_block, slot_block, slot_block],
            out_specs=[head_block, head_block],
        ),
        out_shape=[
            jax.ShapeDtypeStruct((seq_len, width), jnp.bfloat16),
            jax.ShapeDtypeStruct((seq_len, width), jnp.float32),
        ],
    )(count, queries, mate_keys, mate_values)


def attention_backward(count, queries, mate_keys, mate_values, attention_grad, attention, log_total):
    seq_len, width = queries.shape
    heads = width // HD
    head_block = pl.BlockSpec((seq_len, HD), lambda h, c: (0, h))
    slot_block = pl.BlockSpec((SLOTS, seq_len, HD), lambda h, c: (0, 0, 0))
    return pl.pallas_call(
        backward_kernel,
        grid_spec=pltpu.PrefetchScalarGridSpec(
            num_scalar_prefetch=1,
            grid=(heads,),
            in_specs=[head_block, slot_block, slot_block, head_block, head_block, head_block],
            out_specs=[head_block, slot_block, slot_block],
        ),
        out_shape=[
            jax.ShapeDtypeStruct((seq_len, width), jnp.bfloat16),
            jax.ShapeDtypeStruct((SLOTS, seq_len, HD), jnp.float32),
            jax.ShapeDtypeStruct((SLOTS, seq_len, HD), jnp.float32),
        ],
        compiler_params=pltpu.CompilerParams(dimension_semantics=("arbitrary",)),
    )(count, queries, mate_keys, mate_values, attention_grad, attention, log_total)


def exchange(block, axis, bit):
    route = [(low, low ^ (1 << bit)) for low in range(lax.axis_size(axis))]
    return lax.ppermute(block, axis, route)


def bit_reversed(distance):
    return ((distance & 1) << 2) | (distance & 2) | ((distance >> 2) & 1)


def gather_group(block):
    for bit in reversed(range(GROUP.bit_length() - 1)):
        block = jnp.concatenate([block, exchange(block, "resp", bit)], 0)
    return block


def return_group(terms):
    for bit in range(GROUP.bit_length() - 1):
        half = terms.shape[0] // 2
        sent = terms[half:].astype(jnp.bfloat16)
        terms = terms[:half] + exchange(sent, "resp", bit).astype(jnp.float32)
    return terms


def head_sum(row_part):
    heads = lax.axis_size("head")
    total = row_part
    for distance in range(1, heads):
        route = [(low, low ^ distance) for low in range(heads)]
        total = total + lax.ppermute(row_part, "head", route)
    return total


def body(queries, key_states, value_states, partners, counts, norm_gain, out_grad):
    my_index = lax.axis_index("resp")
    seq_len = queries.shape[1]
    mate_rows = bit_reversed(jnp.bitwise_xor(partners[0], my_index))
    count = counts.astype(jnp.int32)
    mate_keys = jnp.take(gather_group(key_states), mate_rows, axis=0)
    mate_values = jnp.take(gather_group(value_states), mate_rows, axis=0)

    attention, log_total = attention_forward(count, queries[0], mate_keys, mate_values)
    attention_flat = attention.astype(jnp.float32)
    scaled_grad = out_grad[0].astype(jnp.float32) * norm_gain
    row_sums = jnp.stack(
        [jnp.sum(attention_flat * attention_flat, -1), jnp.sum(attention_flat * scaled_grad, -1)]
    )
    row_sums = head_sum(row_sums)
    square_sums, dot_sums = row_sums[0], row_sums[1]
    inverse_rms = lax.rsqrt(square_sums / D + EPSILON)
    normed_out = (attention_flat * inverse_rms[:, None] * norm_gain).astype(jnp.bfloat16)[None]
    attention_grad = (
        inverse_rms[:, None] * scaled_grad
        - attention_flat * (inverse_rms**3 * dot_sums / D)[:, None]
    ).astype(jnp.bfloat16)

    query_grads, key_terms, value_terms = attention_backward(
        count, queries[0], mate_keys, mate_values, attention_grad, attention, log_total
    )
    zero_rows = jnp.zeros((GROUP,) + key_terms.shape[1:], jnp.float32)
    key_total = return_group(zero_rows.at[mate_rows].add(key_terms))
    value_total = return_group(zero_rows.at[mate_rows].add(value_terms))
    return (
        normed_out,
        query_grads[None],
        key_total.astype(jnp.bfloat16),
        value_total.astype(jnp.bfloat16),
    )


def solution(mesh):
    placed = (
        P("resp", None, "head"),
        P("resp", None, "head"),
        P("resp", None, "head"),
        P("resp", None),
        P("resp"),
        P("head"),
        P("resp", None, "head"),
    )
    return jax.shard_map(
        body,
        mesh=mesh,
        in_specs=placed,
        out_specs=(
            P("resp", None, "head"),
            P("resp", None, "head"),
            P("resp", None, "head"),
            P("resp", None, "head"),
        ),
        check_vma=False,
    )
```

```python
import functools

import jax
import jax.numpy as jnp
from jax import lax
from jax.experimental import pallas as pl
from jax.experimental.pallas import tpu as pltpu
from jax.sharding import PartitionSpec as P

HD = 128
D = 8192
GROUP = 8
SLOTS = 3
CHUNKS = 2


EPSILON = 1e-05
NEG_FLOOR = -1e30
SCORE_SCALE = HD ** (-0.5)

TRANS_B = (((1,), (1,)), ((), ()))
TRANS_A = (((0,), (0,)), ((), ()))


def slot_scores(count_ref, query_head, mate_keys, slot):
    scores = lax.dot_general(query_head, mate_keys, TRANS_B, preferred_element_type=jnp.float32)
    return jnp.where(slot < count_ref[0], scores * SCORE_SCALE, NEG_FLOOR)


def forward_kernel(count_ref, q_ref, k_ref, v_ref, out_ref, lse_ref):
    query_head = q_ref[...]
    scores = [slot_scores(count_ref, query_head, k_ref[slot], slot) for slot in range(SLOTS)]
    row_max = functools.reduce(
        jnp.maximum, [jnp.max(block, axis=1, keepdims=True) for block in scores]
    )
    exps = [jnp.exp(block - row_max) for block in scores]
    denominator = sum(jnp.sum(block, axis=1, keepdims=True) for block in exps)
    weighted = sum(
        jnp.dot(exps[slot].astype(jnp.bfloat16), v_ref[slot], preferred_element_type=jnp.float32)
        for slot in range(SLOTS)
    )
    out_ref[...] = (weighted / denominator).astype(out_ref.dtype)
    lse_ref[...] = jnp.broadcast_to(row_max + jnp.log(denominator), lse_ref.shape)


def backward_kernel(
    count_ref, q_ref, k_ref, v_ref, grad_ref, att_ref, lse_ref, dk_in, dv_in, dq_ref, dk_ref, dv_ref
):
    @pl.when(pl.program_id(0) == 0)
    def _():
        dk_ref[...] = dk_in[...]
        dv_ref[...] = dv_in[...]

    query_head = q_ref[...]
    grad_head = grad_ref[...]
    row_delta = jnp.sum(
        grad_head.astype(jnp.float32) * att_ref[...].astype(jnp.float32), axis=1, keepdims=True
    )
    log_total = lse_ref[:, :1]
    query_grad = jnp.zeros(dq_ref.shape, jnp.float32)
    for slot in range(SLOTS):
        mate_keys = k_ref[slot]
        back_probs = jnp.exp(slot_scores(count_ref, query_head, mate_keys, slot) - log_total)
        dv_ref[slot] += lax.dot_general(
            back_probs.astype(jnp.bfloat16), grad_head, TRANS_A, preferred_element_type=jnp.float32
        )
        prob_grad = lax.dot_general(
            grad_head, v_ref[slot], TRANS_B, preferred_element_type=jnp.float32
        )
        score_grad = (back_probs * (prob_grad - row_delta)).astype(jnp.bfloat16)
        query_grad = query_grad + jnp.dot(score_grad, mate_keys, preferred_element_type=jnp.float32)
        dk_ref[slot] += SCORE_SCALE * lax.dot_general(
            score_grad, query_head, TRANS_A, preferred_element_type=jnp.float32
        )
    dq_ref[...] = (SCORE_SCALE * query_grad).astype(dq_ref.dtype)


def attention_forward(count, queries, mate_keys, mate_values, chunk, rows):
    seq_len, width = queries.shape
    heads = width // HD
    query_block = pl.BlockSpec((rows, HD), lambda h, c: (chunk, h))
    head_block = pl.BlockSpec((rows, HD), lambda h, c: (0, h))
    slot_block = pl.BlockSpec((SLOTS, seq_len, HD), lambda h, c: (0, 0, 0))
    return pl.pallas_call(
        forward_kernel,
        grid_spec=pltpu.PrefetchScalarGridSpec(
            num_scalar_prefetch=1,
            grid=(heads,),
            in_specs=[query_block, slot_block, slot_block],
            out_specs=[head_block, head_block],
        ),
        out_shape=[
            jax.ShapeDtypeStruct((rows, width), jnp.bfloat16),
            jax.ShapeDtypeStruct((rows, width), jnp.float32),
        ],
    )(count, queries, mate_keys, mate_values)


def attention_backward(
    count, queries, mate_keys, mate_values, attention_grad, attention, log_total, key_part, value_part, chunk
):
    seq_len, width = queries.shape
    rows = attention.shape[0]
    heads = width // HD
    query_block = pl.BlockSpec((rows, HD), lambda h, c: (chunk, h))
    head_block = pl.BlockSpec((rows, HD), lambda h, c: (0, h))
    slot_block = pl.BlockSpec((SLOTS, seq_len, HD), lambda h, c: (0, 0, 0))
    return pl.pallas_call(
        backward_kernel,
        grid_spec=pltpu.PrefetchScalarGridSpec(
            num_scalar_prefetch=1,
            grid=(heads,),
            in_specs=[query_block, slot_block, slot_block, head_block, head_block, head_block]
            + [slot_block, slot_block],
            out_specs=[head_block, slot_block, slot_block],
        ),
        out_shape=[
            jax.ShapeDtypeStruct((rows, width), jnp.bfloat16),
            jax.ShapeDtypeStruct((SLOTS, seq_len, HD), jnp.float32),
            jax.ShapeDtypeStruct((SLOTS, seq_len, HD), jnp.float32),
        ],
        compiler_params=pltpu.CompilerParams(dimension_semantics=("arbitrary",)),
    )(count, queries, mate_keys, mate_values, attention_grad, attention, log_total, key_part, value_part)


def exchange(block, axis, bit):
    route = [(low, low ^ (1 << bit)) for low in range(lax.axis_size(axis))]
    return lax.ppermute(block, axis, route)


def bit_reversed(distance):
    return ((distance & 1) << 2) | (distance & 2) | ((distance >> 2) & 1)


def gather_group(block):
    for bit in reversed(range(GROUP.bit_length() - 1)):
        block = jnp.concatenate([block, exchange(block, "resp", bit)], 0)
    return block


def return_group(terms):
    for bit in range(GROUP.bit_length() - 1):
        half = terms.shape[0] // 2
        sent = terms[half:].astype(jnp.bfloat16)
        terms = terms[:half] + exchange(sent, "resp", bit).astype(jnp.float32)
    return terms


def head_sum(row_part):
    heads = lax.axis_size("head")
    total = row_part
    for distance in range(1, heads):
        route = [(low, low ^ distance) for low in range(heads)]
        total = total + lax.ppermute(row_part, "head", route)
    return total


def body(queries, key_states, value_states, partners, counts, norm_gain, out_grad):
    my_index = lax.axis_index("resp")
    seq_len = queries.shape[1]
    mate_rows = bit_reversed(jnp.bitwise_xor(partners[0], my_index))
    count = counts.astype(jnp.int32)
    mate_keys = jnp.take(gather_group(key_states), mate_rows, axis=0)
    mate_values = jnp.take(gather_group(value_states), mate_rows, axis=0)

    rows = seq_len // CHUNKS
    query_rows = queries[0]
    forward_parts, partial_sums, scaled_parts = [], [], []
    for chunk in range(CHUNKS):
        attention, log_total = attention_forward(count, query_rows, mate_keys, mate_values, chunk, rows)
        attention_flat = attention.astype(jnp.float32)
        scaled_grad = out_grad[0, chunk * rows : (chunk + 1) * rows].astype(jnp.float32) * norm_gain
        row_sums = jnp.stack(
            [jnp.sum(attention_flat * attention_flat, -1), jnp.sum(attention_flat * scaled_grad, -1)]
        )
        row_sums, query_rows = lax.optimization_barrier((row_sums, query_rows))
        forward_parts.append((attention, log_total))
        partial_sums.append(row_sums)
        scaled_parts.append(scaled_grad)
    normed_parts, grad_parts = [], []
    for chunk, (attention, log_total) in enumerate(forward_parts):
        attention_flat = attention.astype(jnp.float32)
        scaled_grad = scaled_parts[chunk]
        row_sums = head_sum(partial_sums[chunk])
        square_sums, dot_sums = row_sums[0], row_sums[1]
        inverse_rms = lax.rsqrt(square_sums / D + EPSILON)
        normed_parts.append((attention_flat * inverse_rms[:, None] * norm_gain).astype(jnp.bfloat16))
        grad_parts.append(
            (
                inverse_rms[:, None] * scaled_grad
                - attention_flat * (inverse_rms**3 * dot_sums / D)[:, None]
            ).astype(jnp.bfloat16)
        )
    normed_out = jnp.concatenate(normed_parts, 0)[None]

    key_terms = jnp.zeros(mate_keys.shape, jnp.float32)
    value_terms = jnp.zeros(mate_values.shape, jnp.float32)
    query_parts = []
    for chunk, (attention, log_total) in enumerate(forward_parts):
        if chunk + 1 < CHUNKS:
            grad_parts[chunk], _ = lax.optimization_barrier((grad_parts[chunk], partial_sums[chunk + 1]))
        query_part, key_terms, value_terms = attention_backward(
            count, queries[0], mate_keys, mate_values, grad_parts[chunk], attention, log_total,
            key_terms, value_terms, chunk,
        )
        query_parts.append(query_part)
    query_grads = jnp.concatenate(query_parts, 0)
    zero_rows = jnp.zeros((GROUP,) + key_terms.shape[1:], jnp.float32)
    key_total = return_group(zero_rows.at[mate_rows].add(key_terms))
    value_total = return_group(zero_rows.at[mate_rows].add(value_terms))
    return (
        normed_out,
        query_grads[None],
        key_total.astype(jnp.bfloat16),
        value_total.astype(jnp.bfloat16),
    )


def solution(mesh):
    placed = (
        P("resp", None, "head"),
        P("resp", None, "head"),
        P("resp", None, "head"),
        P("resp", None),
        P("resp"),
        P("head"),
        P("resp", None, "head"),
    )
    return jax.shard_map(
        body,
        mesh=mesh,
        in_specs=placed,
        out_specs=(
            P("resp", None, "head"),
            P("resp", None, "head"),
            P("resp", None, "head"),
            P("resp", None, "head"),
        ),
        check_vma=False,
    )
```

```python
import functools

import jax
import jax.numpy as jnp
from jax import lax
from jax.experimental import pallas as pl
from jax.experimental.pallas import tpu as pltpu
from jax.sharding import PartitionSpec as P

HD = 128
D = 8192
GROUP = 8
SLOTS = 3


EPSILON = 1e-05
NEG_FLOOR = -1e30
SCORE_SCALE = HD ** (-0.5)

TRANS_B = (((1,), (1,)), ((), ()))
TRANS_A = (((0,), (0,)), ((), ()))


def slot_scores(count_ref, query_head, mate_keys, slot):
    scores = lax.dot_general(query_head, mate_keys, TRANS_B, preferred_element_type=jnp.float32)
    return jnp.where(slot < count_ref[0], scores * SCORE_SCALE, NEG_FLOOR)


def forward_kernel(count_ref, rows_ref, q_ref, *refs):
    k_refs, v_refs, (out_ref, lse_ref) = refs[:SLOTS], refs[SLOTS : 2 * SLOTS], refs[2 * SLOTS :]
    query_head = q_ref[...]
    scores = [slot_scores(count_ref, query_head, k_refs[slot][...], slot) for slot in range(SLOTS)]
    row_max = functools.reduce(
        jnp.maximum, [jnp.max(block, axis=1, keepdims=True) for block in scores]
    )
    exps = [jnp.exp(block - row_max) for block in scores]
    denominator = sum(jnp.sum(block, axis=1, keepdims=True) for block in exps)
    weighted = sum(
        jnp.dot(exps[slot].astype(jnp.bfloat16), v_refs[slot][...], preferred_element_type=jnp.float32)
        for slot in range(SLOTS)
    )
    out_ref[...] = (weighted / denominator).astype(out_ref.dtype)
    lse_ref[...] = jnp.broadcast_to(row_max + jnp.log(denominator), lse_ref.shape)


def backward_kernel(count_ref, rows_ref, q_ref, *refs):
    k_refs, v_refs = refs[:SLOTS], refs[SLOTS : 2 * SLOTS]
    grad_ref, att_ref, lse_ref, dq_ref, dk_ref, dv_ref = refs[2 * SLOTS :]

    @pl.when(pl.program_id(0) == 0)
    def _():
        dk_ref[...] = jnp.zeros_like(dk_ref)
        dv_ref[...] = jnp.zeros_like(dv_ref)

    query_head = q_ref[...]
    grad_head = grad_ref[...]
    row_delta = jnp.sum(
        grad_head.astype(jnp.float32) * att_ref[...].astype(jnp.float32), axis=1, keepdims=True
    )
    log_total = lse_ref[:, :1]
    query_grad = jnp.zeros(dq_ref.shape, jnp.float32)
    for slot in range(SLOTS):
        mate_keys = k_refs[slot][...]
        mate_row = rows_ref[slot]
        back_probs = jnp.exp(slot_scores(count_ref, query_head, mate_keys, slot) - log_total)
        dv_ref[mate_row] += lax.dot_general(
            back_probs.astype(jnp.bfloat16), grad_head, TRANS_A, preferred_element_type=jnp.float32
        )
        prob_grad = lax.dot_general(
            grad_head, v_refs[slot][...], TRANS_B, preferred_element_type=jnp.float32
        )
        score_grad = (back_probs * (prob_grad - row_delta)).astype(jnp.bfloat16)
        query_grad = query_grad + jnp.dot(score_grad, mate_keys, preferred_element_type=jnp.float32)
        dk_ref[mate_row] += SCORE_SCALE * lax.dot_general(
            score_grad, query_head, TRANS_A, preferred_element_type=jnp.float32
        )
    dq_ref[...] = (SCORE_SCALE * query_grad).astype(dq_ref.dtype)


def slot_blocks(seq_len):
    return [
        pl.BlockSpec((None, seq_len, HD), lambda h, c, r, slot=slot: (r[slot], 0, 0))
        for slot in range(SLOTS)
    ]


def attention_forward(count, mate_rows, queries, group_keys, group_values):
    seq_len, width = queries.shape
    heads = width // HD
    head_block = pl.BlockSpec((seq_len, HD), lambda h, c, r: (0, h))
    return pl.pallas_call(
        forward_kernel,
        grid_spec=pltpu.PrefetchScalarGridSpec(
            num_scalar_prefetch=2,
            grid=(heads,),
            in_specs=[head_block] + slot_blocks(seq_len) * 2,
            out_specs=[head_block, head_block],
        ),
        out_shape=[
            jax.ShapeDtypeStruct((seq_len, width), jnp.bfloat16),
            jax.ShapeDtypeStruct((seq_len, width), jnp.float32),
        ],
    )(count, mate_rows, queries, *([group_keys] * SLOTS), *([group_values] * SLOTS))


def attention_backward(
    count, mate_rows, queries, group_keys, group_values, attention_grad, attention, log_total
):
    seq_len, width = queries.shape
    heads = width // HD
    head_block = pl.BlockSpec((seq_len, HD), lambda h, c, r: (0, h))
    group_block = pl.BlockSpec(group_keys.shape, lambda h, c, r: (0, 0, 0))
    return pl.pallas_call(
        backward_kernel,
        grid_spec=pltpu.PrefetchScalarGridSpec(
            num_scalar_prefetch=2,
            grid=(heads,),
            in_specs=[head_block] + slot_blocks(seq_len) * 2 + [head_block] * 3,
            out_specs=[head_block, group_block, group_block],
        ),
        out_shape=[
            jax.ShapeDtypeStruct((seq_len, width), jnp.bfloat16),
            jax.ShapeDtypeStruct(group_keys.shape, jnp.float32),
            jax.ShapeDtypeStruct(group_keys.shape, jnp.float32),
        ],
        compiler_params=pltpu.CompilerParams(dimension_semantics=("arbitrary",)),
    )(
        count, mate_rows, queries, *([group_keys] * SLOTS), *([group_values] * SLOTS),
        attention_grad, attention, log_total,
    )


def exchange(block, axis, bit):
    route = [(low, low ^ (1 << bit)) for low in range(lax.axis_size(axis))]
    return lax.ppermute(block, axis, route)


def bit_reversed(distance):
    return ((distance & 1) << 2) | (distance & 2) | ((distance >> 2) & 1)


def gather_group(block):
    for bit in reversed(range(GROUP.bit_length() - 1)):
        block = jnp.concatenate([block, exchange(block, "resp", bit)], 0)
    return block


def return_group(terms):
    for bit in range(GROUP.bit_length() - 1):
        half = terms.shape[0] // 2
        sent = terms[half:].astype(jnp.bfloat16)
        terms = terms[:half] + exchange(sent, "resp", bit).astype(jnp.float32)
    return terms


def head_sum(row_part):
    heads = lax.axis_size("head")
    total = row_part
    for distance in range(1, heads):
        route = [(low, low ^ distance) for low in range(heads)]
        total = total + lax.ppermute(row_part, "head", route)
    return total


def body(queries, key_states, value_states, partners, counts, norm_gain, out_grad):
    my_index = lax.axis_index("resp")
    seq_len = queries.shape[1]
    mate_rows = bit_reversed(jnp.bitwise_xor(partners[0], my_index))
    count = counts.astype(jnp.int32)
    group_keys = gather_group(key_states)
    group_values = gather_group(value_states)

    attention, log_total = attention_forward(count, mate_rows, queries[0], group_keys, group_values)
    attention_flat = attention.astype(jnp.float32)
    scaled_grad = out_grad[0].astype(jnp.float32) * norm_gain
    row_sums = jnp.stack(
        [jnp.sum(attention_flat * attention_flat, -1), jnp.sum(attention_flat * scaled_grad, -1)]
    )
    row_sums = head_sum(row_sums)
    square_sums, dot_sums = row_sums[0], row_sums[1]
    inverse_rms = lax.rsqrt(square_sums / D + EPSILON)
    normed_out = (attention_flat * inverse_rms[:, None] * norm_gain).astype(jnp.bfloat16)[None]
    attention_grad = (
        inverse_rms[:, None] * scaled_grad
        - attention_flat * (inverse_rms**3 * dot_sums / D)[:, None]
    ).astype(jnp.bfloat16)

    query_grads, key_terms, value_terms = attention_backward(
        count, mate_rows, queries[0], group_keys, group_values, attention_grad, attention, log_total
    )
    key_total = return_group(key_terms)
    value_total = return_group(value_terms)
    return (
        normed_out,
        query_grads[None],
        key_total.astype(jnp.bfloat16),
        value_total.astype(jnp.bfloat16),
    )


def solution(mesh):
    placed = (
        P("resp", None, "head"),
        P("resp", None, "head"),
        P("resp", None, "head"),
        P("resp", None),
        P("resp"),
        P("head"),
        P("resp", None, "head"),
    )
    return jax.shard_map(
        body,
        mesh=mesh,
        in_specs=placed,
        out_specs=(
            P("resp", None, "head"),
            P("resp", None, "head"),
            P("resp", None, "head"),
            P("resp", None, "head"),
        ),
        check_vma=False,
    )
```

```python
import functools

import jax
import jax.numpy as jnp
from jax import lax
from jax.experimental import pallas as pl
from jax.experimental.pallas import tpu as pltpu
from jax.sharding import PartitionSpec as P

HD = 128
D = 8192
GROUP = 8
SLOTS = 3


EPSILON = 1e-05
NEG_FLOOR = -1e30
SCORE_SCALE = HD ** (-0.5)

TRANS_B = (((1,), (1,)), ((), ()))
TRANS_A = (((0,), (0,)), ((), ()))


def slot_scores(count_ref, query_head, mate_keys, slot):
    scores = lax.dot_general(query_head, mate_keys, TRANS_B, preferred_element_type=jnp.float32)
    return jnp.where(slot < count_ref[0], scores * SCORE_SCALE, NEG_FLOOR)


def forward_kernel(count_ref, q_ref, k_ref, v_ref, out_ref, lse_ref):
    query_head = q_ref[...]
    scores = [slot_scores(count_ref, query_head, k_ref[slot], slot) for slot in range(SLOTS)]
    row_max = functools.reduce(
        jnp.maximum, [jnp.max(block, axis=1, keepdims=True) for block in scores]
    )
    exps = [jnp.exp(block - row_max) for block in scores]
    denominator = sum(jnp.sum(block, axis=1, keepdims=True) for block in exps)
    weighted = sum(
        jnp.dot(exps[slot].astype(jnp.bfloat16), v_ref[slot], preferred_element_type=jnp.float32)
        for slot in range(SLOTS)
    )
    out_ref[...] = (weighted / denominator).astype(out_ref.dtype)
    lse_ref[...] = jnp.broadcast_to(row_max + jnp.log(denominator), lse_ref.shape)


def backward_kernel(
    count_ref, q_ref, k_ref, v_ref, grad_ref, lse_ref, delta_ref, dq_ref, dk_ref, dv_ref
):
    @pl.when(pl.program_id(0) == 0)
    def _():
        dk_ref[...] = jnp.zeros_like(dk_ref)
        dv_ref[...] = jnp.zeros_like(dv_ref)

    query_head = q_ref[...]
    grad_head = grad_ref[...]
    log_total = lse_ref[...]
    row_delta = delta_ref[...]
    query_grad = jnp.zeros(dq_ref.shape, jnp.float32)
    for slot in range(SLOTS):
        mate_keys = k_ref[slot]
        back_probs = jnp.exp(slot_scores(count_ref, mate_keys, query_head, slot) - log_total)
        dv_ref[slot] += jnp.dot(
            back_probs.astype(jnp.bfloat16), grad_head, preferred_element_type=jnp.float32
        )
        prob_grad = lax.dot_general(
            v_ref[slot], grad_head, TRANS_B, preferred_element_type=jnp.float32
        )
        score_grad = (back_probs * (prob_grad - row_delta)).astype(jnp.bfloat16)
        dk_ref[slot] += SCORE_SCALE * jnp.dot(
            score_grad, query_head, preferred_element_type=jnp.float32
        )
        query_grad = query_grad + lax.dot_general(
            score_grad, mate_keys, TRANS_A, preferred_element_type=jnp.float32
        )
    dq_ref[...] = (SCORE_SCALE * query_grad).astype(dq_ref.dtype)


def attention_forward(count, queries, mate_keys, mate_values):
    seq_len, width = queries.shape
    heads = width // HD
    head_block = pl.BlockSpec((seq_len, HD), lambda h, c: (0, h))
    slot_block = pl.BlockSpec((SLOTS, seq_len, HD), lambda h, c: (0, 0, 0))
    return pl.pallas_call(
        forward_kernel,
        grid_spec=pltpu.PrefetchScalarGridSpec(
            num_scalar_prefetch=1,
            grid=(heads,),
            in_specs=[head_block, slot_block, slot_block],
            out_specs=[head_block, head_block],
        ),
        out_shape=[
            jax.ShapeDtypeStruct((seq_len, width), jnp.bfloat16),
            jax.ShapeDtypeStruct((seq_len, width), jnp.float32),
        ],
    )(count, queries, mate_keys, mate_values)


def attention_backward(count, queries, mate_keys, mate_values, attention_grad, log_rows, delta_rows):
    seq_len, width = queries.shape
    heads = width // HD
    head_block = pl.BlockSpec((seq_len, HD), lambda h, c: (0, h))
    row_block = pl.BlockSpec((None, 1, seq_len), lambda h, c: (h, 0, 0))
    slot_block = pl.BlockSpec((SLOTS, seq_len, HD), lambda h, c: (0, 0, 0))
    return pl.pallas_call(
        backward_kernel,
        grid_spec=pltpu.PrefetchScalarGridSpec(
            num_scalar_prefetch=1,
            grid=(heads,),
            in_specs=[head_block, slot_block, slot_block, head_block, row_block, row_block],
            out_specs=[head_block, slot_block, slot_block],
        ),
        out_shape=[
            jax.ShapeDtypeStruct((seq_len, width), jnp.bfloat16),
            jax.ShapeDtypeStruct((SLOTS, seq_len, HD), jnp.float32),
            jax.ShapeDtypeStruct((SLOTS, seq_len, HD), jnp.float32),
        ],
        compiler_params=pltpu.CompilerParams(dimension_semantics=("arbitrary",)),
    )(count, queries, mate_keys, mate_values, attention_grad, log_rows, delta_rows)


def exchange(block, axis, bit):
    route = [(low, low ^ (1 << bit)) for low in range(lax.axis_size(axis))]
    return lax.ppermute(block, axis, route)


def bit_reversed(distance):
    return ((distance & 1) << 2) | (distance & 2) | ((distance >> 2) & 1)


def gather_group(block):
    for bit in reversed(range(GROUP.bit_length() - 1)):
        block = jnp.concatenate([block, exchange(block, "resp", bit)], 0)
    return block


def return_group(terms):
    for bit in range(GROUP.bit_length() - 1):
        half = terms.shape[0] // 2
        sent = terms[half:].astype(jnp.bfloat16)
        terms = terms[:half] + exchange(sent, "resp", bit).astype(jnp.float32)
    return terms


def head_sum(row_part):
    heads = lax.axis_size("head")
    total = row_part
    for distance in range(1, heads):
        route = [(low, low ^ distance) for low in range(heads)]
        total = total + lax.ppermute(row_part, "head", route)
    return total


def body(queries, key_states, value_states, partners, counts, norm_gain, out_grad):
    my_index = lax.axis_index("resp")
    seq_len = queries.shape[1]
    mate_rows = bit_reversed(jnp.bitwise_xor(partners[0], my_index))
    count = counts.astype(jnp.int32)
    mate_keys = jnp.take(gather_group(key_states), mate_rows, axis=0)
    mate_values = jnp.take(gather_group(value_states), mate_rows, axis=0)

    attention, log_total = attention_forward(count, queries[0], mate_keys, mate_values)
    attention_flat = attention.astype(jnp.float32)
    scaled_grad = out_grad[0].astype(jnp.float32) * norm_gain
    row_sums = jnp.stack(
        [jnp.sum(attention_flat * attention_flat, -1), jnp.sum(attention_flat * scaled_grad, -1)]
    )
    row_sums = head_sum(row_sums)
    square_sums, dot_sums = row_sums[0], row_sums[1]
    inverse_rms = lax.rsqrt(square_sums / D + EPSILON)
    normed_out = (attention_flat * inverse_rms[:, None] * norm_gain).astype(jnp.bfloat16)[None]
    attention_grad = (
        inverse_rms[:, None] * scaled_grad
        - attention_flat * (inverse_rms**3 * dot_sums / D)[:, None]
    ).astype(jnp.bfloat16)

    heads = attention.shape[1] // HD
    log_rows = log_total[:, ::HD].T.reshape(heads, 1, seq_len)
    delta_rows = jnp.sum(
        (attention_grad.astype(jnp.float32) * attention_flat).reshape(seq_len, heads, HD), -1
    ).T.reshape(heads, 1, seq_len)
    query_grads, key_terms, value_terms = attention_backward(
        count, queries[0], mate_keys, mate_values, attention_grad, log_rows, delta_rows
    )
    zero_rows = jnp.zeros((GROUP,) + key_terms.shape[1:], jnp.float32)
    key_total = return_group(zero_rows.at[mate_rows].add(key_terms))
    value_total = return_group(zero_rows.at[mate_rows].add(value_terms))
    return (
        normed_out,
        query_grads[None],
        key_total.astype(jnp.bfloat16),
        value_total.astype(jnp.bfloat16),
    )


def solution(mesh):
    placed = (
        P("resp", None, "head"),
        P("resp", None, "head"),
        P("resp", None, "head"),
        P("resp", None),
        P("resp"),
        P("head"),
        P("resp", None, "head"),
    )
    return jax.shard_map(
        body,
        mesh=mesh,
        in_specs=placed,
        out_specs=(
            P("resp", None, "head"),
            P("resp", None, "head"),
            P("resp", None, "head"),
            P("resp", None, "head"),
        ),
        check_vma=False,
    )
```

```python
import functools

import jax
import jax.numpy as jnp
from jax import lax
from jax.experimental import pallas as pl
from jax.experimental.pallas import tpu as pltpu
from jax.sharding import PartitionSpec as P

HD = 128
D = 8192
GROUP = 8
SLOTS = 3


EPSILON = 1e-05
NEG_FLOOR = -1e30
SCORE_SCALE = HD ** (-0.5)

TRANS_B = (((1,), (1,)), ((), ()))
TRANS_A = (((0,), (0,)), ((), ()))


def slot_scores(count_ref, query_head, mate_keys, slot):
    scores = lax.dot_general(query_head, mate_keys, TRANS_B, preferred_element_type=jnp.float32)
    return jnp.where(slot < count_ref[0], scores * SCORE_SCALE, NEG_FLOOR)


def as_lane_row(column):
    return jnp.transpose(jnp.broadcast_to(column, (column.shape[0], HD)))[:1]


def forward_kernel(count_ref, q_ref, k_ref, v_ref, out_ref, lse_ref):
    query_head = q_ref[...]
    scores = [slot_scores(count_ref, query_head, k_ref[slot], slot) for slot in range(SLOTS)]
    row_max = functools.reduce(
        jnp.maximum, [jnp.max(block, axis=1, keepdims=True) for block in scores]
    )
    exps = [jnp.exp(block - row_max) for block in scores]
    denominator = sum(jnp.sum(block, axis=1, keepdims=True) for block in exps)
    weighted = sum(
        jnp.dot(exps[slot].astype(jnp.bfloat16), v_ref[slot], preferred_element_type=jnp.float32)
        for slot in range(SLOTS)
    )
    out_ref[...] = (weighted / denominator).astype(out_ref.dtype)
    lse_ref[...] = as_lane_row(row_max + jnp.log(denominator))


def backward_kernel(
    count_ref, q_ref, k_ref, v_ref, grad_ref, att_ref, lse_ref, dq_ref, dk_ref, dv_ref
):
    @pl.when(pl.program_id(0) == 0)
    def _():
        dk_ref[...] = jnp.zeros_like(dk_ref)
        dv_ref[...] = jnp.zeros_like(dv_ref)

    query_head = q_ref[...]
    grad_head = grad_ref[...]
    log_total = lse_ref[...]
    row_delta = as_lane_row(
        jnp.sum(grad_head.astype(jnp.float32) * att_ref[...].astype(jnp.float32), axis=1, keepdims=True)
    )
    query_grad = jnp.zeros(dq_ref.shape, jnp.float32)
    for slot in range(SLOTS):
        mate_keys = k_ref[slot]
        back_probs = jnp.exp(slot_scores(count_ref, mate_keys, query_head, slot) - log_total)
        dv_ref[slot] += jnp.dot(
            back_probs.astype(jnp.bfloat16), grad_head, preferred_element_type=jnp.float32
        )
        prob_grad = lax.dot_general(
            v_ref[slot], grad_head, TRANS_B, preferred_element_type=jnp.float32
        )
        score_grad = (back_probs * (prob_grad - row_delta)).astype(jnp.bfloat16)
        dk_ref[slot] += SCORE_SCALE * jnp.dot(
            score_grad, query_head, preferred_element_type=jnp.float32
        )
        query_grad = query_grad + lax.dot_general(
            score_grad, mate_keys, TRANS_A, preferred_element_type=jnp.float32
        )
    dq_ref[...] = (SCORE_SCALE * query_grad).astype(dq_ref.dtype)


def attention_forward(count, queries, mate_keys, mate_values):
    seq_len, width = queries.shape
    heads = width // HD
    head_block = pl.BlockSpec((seq_len, HD), lambda h, c: (0, h))
    slot_block = pl.BlockSpec((SLOTS, seq_len, HD), lambda h, c: (0, 0, 0))
    return pl.pallas_call(
        forward_kernel,
        grid_spec=pltpu.PrefetchScalarGridSpec(
            num_scalar_prefetch=1,
            grid=(heads,),
            in_specs=[head_block, slot_block, slot_block],
            out_specs=[head_block, pl.BlockSpec((None, 1, seq_len), lambda h, c: (h, 0, 0))],
        ),
        out_shape=[
            jax.ShapeDtypeStruct((seq_len, width), jnp.bfloat16),
            jax.ShapeDtypeStruct((heads, 1, seq_len), jnp.float32),
        ],
    )(count, queries, mate_keys, mate_values)


def attention_backward(count, queries, mate_keys, mate_values, attention_grad, attention, log_rows):
    seq_len, width = queries.shape
    heads = width // HD
    head_block = pl.BlockSpec((seq_len, HD), lambda h, c: (0, h))
    row_block = pl.BlockSpec((None, 1, seq_len), lambda h, c: (h, 0, 0))
    slot_block = pl.BlockSpec((SLOTS, seq_len, HD), lambda h, c: (0, 0, 0))
    return pl.pallas_call(
        backward_kernel,
        grid_spec=pltpu.PrefetchScalarGridSpec(
            num_scalar_prefetch=1,
            grid=(heads,),
            in_specs=[head_block, slot_block, slot_block, head_block, head_block, row_block],
            out_specs=[head_block, slot_block, slot_block],
        ),
        out_shape=[
            jax.ShapeDtypeStruct((seq_len, width), jnp.bfloat16),
            jax.ShapeDtypeStruct((SLOTS, seq_len, HD), jnp.float32),
            jax.ShapeDtypeStruct((SLOTS, seq_len, HD), jnp.float32),
        ],
        compiler_params=pltpu.CompilerParams(dimension_semantics=("arbitrary",)),
    )(count, queries, mate_keys, mate_values, attention_grad, attention, log_rows)


def exchange(block, axis, bit):
    route = [(low, low ^ (1 << bit)) for low in range(lax.axis_size(axis))]
    return lax.ppermute(block, axis, route)


def bit_reversed(distance):
    return ((distance & 1) << 2) | (distance & 2) | ((distance >> 2) & 1)


def gather_group(block):
    for bit in reversed(range(GROUP.bit_length() - 1)):
        block = jnp.concatenate([block, exchange(block, "resp", bit)], 0)
    return block


def return_group(terms):
    for bit in range(GROUP.bit_length() - 1):
        half = terms.shape[0] // 2
        sent = terms[half:].astype(jnp.bfloat16)
        terms = terms[:half] + exchange(sent, "resp", bit).astype(jnp.float32)
    return terms


def head_sum(row_part):
    heads = lax.axis_size("head")
    total = row_part
    for distance in range(1, heads):
        route = [(low, low ^ distance) for low in range(heads)]
        total = total + lax.ppermute(row_part, "head", route)
    return total


def body(queries, key_states, value_states, partners, counts, norm_gain, out_grad):
    my_index = lax.axis_index("resp")
    seq_len = queries.shape[1]
    mate_rows = bit_reversed(jnp.bitwise_xor(partners[0], my_index))
    count = counts.astype(jnp.int32)
    mate_keys = jnp.take(gather_group(key_states), mate_rows, axis=0)
    mate_values = jnp.take(gather_group(value_states), mate_rows, axis=0)

    attention, log_total = attention_forward(count, queries[0], mate_keys, mate_values)
    attention_flat = attention.astype(jnp.float32)
    scaled_grad = out_grad[0].astype(jnp.float32) * norm_gain
    row_sums = jnp.stack(
        [jnp.sum(attention_flat * attention_flat, -1), jnp.sum(attention_flat * scaled_grad, -1)]
    )
    row_sums = head_sum(row_sums)
    square_sums, dot_sums = row_sums[0], row_sums[1]
    inverse_rms = lax.rsqrt(square_sums / D + EPSILON)
    normed_out = (attention_flat * inverse_rms[:, None] * norm_gain).astype(jnp.bfloat16)[None]
    attention_grad = (
        inverse_rms[:, None] * scaled_grad
        - attention_flat * (inverse_rms**3 * dot_sums / D)[:, None]
    ).astype(jnp.bfloat16)

    query_grads, key_terms, value_terms = attention_backward(
        count, queries[0], mate_keys, mate_values, attention_grad, attention, log_total
    )
    zero_rows = jnp.zeros((GROUP,) + key_terms.shape[1:], jnp.float32)
    key_total = return_group(zero_rows.at[mate_rows].add(key_terms))
    value_total = return_group(zero_rows.at[mate_rows].add(value_terms))
    return (
        normed_out,
        query_grads[None],
        key_total.astype(jnp.bfloat16),
        value_total.astype(jnp.bfloat16),
    )


def solution(mesh):
    placed = (
        P("resp", None, "head"),
        P("resp", None, "head"),
        P("resp", None, "head"),
        P("resp", None),
        P("resp"),
        P("head"),
        P("resp", None, "head"),
    )
    return jax.shard_map(
        body,
        mesh=mesh,
        in_specs=placed,
        out_specs=(
            P("resp", None, "head"),
            P("resp", None, "head"),
            P("resp", None, "head"),
            P("resp", None, "head"),
        ),
        check_vma=False,
    )
```

```python
import functools

import jax
import jax.numpy as jnp
from jax import lax
from jax.experimental import pallas as pl
from jax.experimental.pallas import tpu as pltpu
from jax.sharding import PartitionSpec as P

HD = 128
D = 8192
GROUP = 8
SLOTS = 3


EPSILON = 1e-05
SCORE_SCALE = HD ** (-0.5)

TRANS_B = (((1,), (1,)), ((), ()))
TRANS_A = (((0,), (0,)), ((), ()))


def slot_scores(query_head, mate_keys):
    scores = lax.dot_general(query_head, mate_keys, TRANS_B, preferred_element_type=jnp.float32)
    return scores * SCORE_SCALE


def slot_offset(count_ref, slot, offset, dead):
    return jnp.where(slot < count_ref[0], offset, dead)


def as_lane_row(column):
    return jnp.transpose(jnp.broadcast_to(column, (column.shape[0], HD)))[:1]


def forward_kernel(count_ref, q_ref, k_ref, v_ref, out_ref, lse_ref):
    query_head = q_ref[...]
    scores = [slot_scores(query_head, k_ref[slot]) for slot in range(SLOTS)]
    row_max = functools.reduce(
        jnp.maximum,
        [
            slot_offset(count_ref, slot, jnp.max(block, axis=1, keepdims=True), -jnp.inf)
            for slot, block in enumerate(scores)
        ],
    )
    exps = [
        jnp.exp(block - slot_offset(count_ref, slot, row_max, jnp.inf))
        for slot, block in enumerate(scores)
    ]
    denominator = sum(jnp.sum(block, axis=1, keepdims=True) for block in exps)
    weighted = sum(
        jnp.dot(exps[slot].astype(jnp.bfloat16), v_ref[slot], preferred_element_type=jnp.float32)
        for slot in range(SLOTS)
    )
    out_ref[...] = (weighted / denominator).astype(out_ref.dtype)
    lse_ref[...] = as_lane_row(row_max + jnp.log(denominator))


def backward_kernel(
    count_ref, q_ref, k_ref, v_ref, grad_ref, att_ref, lse_ref, dq_ref, dk_ref, dv_ref
):
    @pl.when(pl.program_id(0) == 0)
    def _():
        dk_ref[...] = jnp.zeros_like(dk_ref)
        dv_ref[...] = jnp.zeros_like(dv_ref)

    query_head = q_ref[...]
    grad_head = grad_ref[...]
    log_total = lse_ref[...]
    row_delta = as_lane_row(
        jnp.sum(grad_head.astype(jnp.float32) * att_ref[...].astype(jnp.float32), axis=1, keepdims=True)
    )
    query_grad = jnp.zeros(dq_ref.shape, jnp.float32)
    for slot in range(SLOTS):
        mate_keys = k_ref[slot]
        back_probs = jnp.exp(
            slot_scores(mate_keys, query_head) - slot_offset(count_ref, slot, log_total, jnp.inf)
        )
        dv_ref[slot] += jnp.dot(
            back_probs.astype(jnp.bfloat16), grad_head, preferred_element_type=jnp.float32
        )
        prob_grad = lax.dot_general(
            v_ref[slot], grad_head, TRANS_B, preferred_element_type=jnp.float32
        )
        score_grad = (back_probs * (prob_grad - row_delta)).astype(jnp.bfloat16)
        dk_ref[slot] += SCORE_SCALE * jnp.dot(
            score_grad, query_head, preferred_element_type=jnp.float32
        )
        query_grad = query_grad + lax.dot_general(
            score_grad, mate_keys, TRANS_A, preferred_element_type=jnp.float32
        )
    dq_ref[...] = (SCORE_SCALE * query_grad).astype(dq_ref.dtype)


def attention_forward(count, queries, mate_keys, mate_values):
    seq_len, width = queries.shape
    heads = width // HD
    head_block = pl.BlockSpec((seq_len, HD), lambda h, c: (0, h))
    slot_block = pl.BlockSpec((SLOTS, seq_len, HD), lambda h, c: (0, 0, 0))
    return pl.pallas_call(
        forward_kernel,
        grid_spec=pltpu.PrefetchScalarGridSpec(
            num_scalar_prefetch=1,
            grid=(heads,),
            in_specs=[head_block, slot_block, slot_block],
            out_specs=[head_block, pl.BlockSpec((None, 1, seq_len), lambda h, c: (h, 0, 0))],
        ),
        out_shape=[
            jax.ShapeDtypeStruct((seq_len, width), jnp.bfloat16),
            jax.ShapeDtypeStruct((heads, 1, seq_len), jnp.float32),
        ],
    )(count, queries, mate_keys, mate_values)


def attention_backward(count, queries, mate_keys, mate_values, attention_grad, attention, log_rows):
    seq_len, width = queries.shape
    heads = width // HD
    head_block = pl.BlockSpec((seq_len, HD), lambda h, c: (0, h))
    row_block = pl.BlockSpec((None, 1, seq_len), lambda h, c: (h, 0, 0))
    slot_block = pl.BlockSpec((SLOTS, seq_len, HD), lambda h, c: (0, 0, 0))
    return pl.pallas_call(
        backward_kernel,
        grid_spec=pltpu.PrefetchScalarGridSpec(
            num_scalar_prefetch=1,
            grid=(heads,),
            in_specs=[head_block, slot_block, slot_block, head_block, head_block, row_block],
            out_specs=[head_block, slot_block, slot_block],
        ),
        out_shape=[
            jax.ShapeDtypeStruct((seq_len, width), jnp.bfloat16),
            jax.ShapeDtypeStruct((SLOTS, seq_len, HD), jnp.float32),
            jax.ShapeDtypeStruct((SLOTS, seq_len, HD), jnp.float32),
        ],
        compiler_params=pltpu.CompilerParams(dimension_semantics=("arbitrary",)),
    )(count, queries, mate_keys, mate_values, attention_grad, attention, log_rows)


def exchange(block, axis, bit):
    route = [(low, low ^ (1 << bit)) for low in range(lax.axis_size(axis))]
    return lax.ppermute(block, axis, route)


def bit_reversed(distance):
    return ((distance & 1) << 2) | (distance & 2) | ((distance >> 2) & 1)


def gather_group(block):
    for bit in reversed(range(GROUP.bit_length() - 1)):
        block = jnp.concatenate([block, exchange(block, "resp", bit)], 0)
    return block


def return_group(terms):
    for bit in range(GROUP.bit_length() - 1):
        half = terms.shape[0] // 2
        sent = terms[half:].astype(jnp.bfloat16)
        terms = terms[:half] + exchange(sent, "resp", bit).astype(jnp.float32)
    return terms


def head_sum(row_part):
    for bit in range(lax.axis_size("head").bit_length() - 1):
        row_part = row_part + exchange(row_part, "head", bit)
    return row_part


def body(queries, key_states, value_states, partners, counts, norm_gain, out_grad):
    my_index = lax.axis_index("resp")
    seq_len = queries.shape[1]
    mate_rows = bit_reversed(jnp.bitwise_xor(partners[0], my_index))
    count = counts.astype(jnp.int32)
    mate_keys = jnp.take(gather_group(key_states), mate_rows, axis=0)
    mate_values = jnp.take(gather_group(value_states), mate_rows, axis=0)

    attention, log_total = attention_forward(count, queries[0], mate_keys, mate_values)
    attention_flat = attention.astype(jnp.float32)
    scaled_grad = out_grad[0].astype(jnp.float32) * norm_gain
    row_sums = jnp.stack(
        [jnp.sum(attention_flat * attention_flat, -1), jnp.sum(attention_flat * scaled_grad, -1)]
    )
    row_sums = head_sum(row_sums)
    square_sums, dot_sums = row_sums[0], row_sums[1]
    inverse_rms = lax.rsqrt(square_sums / D + EPSILON)
    normed_out = (attention_flat * inverse_rms[:, None] * norm_gain).astype(jnp.bfloat16)[None]
    attention_grad = (
        inverse_rms[:, None] * scaled_grad
        - attention_flat * (inverse_rms**3 * dot_sums / D)[:, None]
    ).astype(jnp.bfloat16)

    query_grads, key_terms, value_terms = attention_backward(
        count, queries[0], mate_keys, mate_values, attention_grad, attention, log_total
    )
    zero_rows = jnp.zeros((GROUP,) + key_terms.shape[1:], jnp.float32)
    key_total = return_group(zero_rows.at[mate_rows].add(key_terms))
    value_total = return_group(zero_rows.at[mate_rows].add(value_terms))
    return (
        normed_out,
        query_grads[None],
        key_total.astype(jnp.bfloat16),
        value_total.astype(jnp.bfloat16),
    )


def solution(mesh):
    placed = (
        P("resp", None, "head"),
        P("resp", None, "head"),
        P("resp", None, "head"),
        P("resp", None),
        P("resp"),
        P("head"),
        P("resp", None, "head"),
    )
    return jax.shard_map(
        body,
        mesh=mesh,
        in_specs=placed,
        out_specs=(
            P("resp", None, "head"),
            P("resp", None, "head"),
            P("resp", None, "head"),
            P("resp", None, "head"),
        ),
        check_vma=False,
    )
```

```python
import functools

import jax
import jax.numpy as jnp
from jax import lax
from jax.experimental import pallas as pl
from jax.experimental.pallas import tpu as pltpu
from jax.sharding import PartitionSpec as P

HD = 128
D = 8192
GROUP = 8
SLOTS = 3


EPSILON = 1e-05
SCORE_SCALE = HD ** (-0.5)

TRANS_B = (((1,), (1,)), ((), ()))
TRANS_A = (((0,), (0,)), ((), ()))


def slot_scores(query_head, mate_keys):
    scores = lax.dot_general(query_head, mate_keys, TRANS_B, preferred_element_type=jnp.float32)
    return scores * SCORE_SCALE


def slot_offset(count_ref, slot, offset, dead):
    return jnp.where(slot < count_ref[0], offset, dead)


def as_lane_row(column):
    return jnp.transpose(jnp.broadcast_to(column, (column.shape[0], HD)))[:1]


def forward_kernel(count_ref, q_ref, k_ref, v_ref, out_ref, lse_ref):
    query_head = q_ref[...]
    scores = [slot_scores(query_head, k_ref[slot]) for slot in range(SLOTS)]
    row_max = functools.reduce(
        jnp.maximum,
        [
            slot_offset(count_ref, slot, jnp.max(block, axis=1, keepdims=True), -jnp.inf)
            for slot, block in enumerate(scores)
        ],
    )
    exps = [
        jnp.exp(block - slot_offset(count_ref, slot, row_max, jnp.inf))
        for slot, block in enumerate(scores)
    ]
    denominator = sum(jnp.sum(block, axis=1, keepdims=True) for block in exps)
    weighted = sum(
        jnp.dot(exps[slot].astype(jnp.bfloat16), v_ref[slot], preferred_element_type=jnp.float32)
        for slot in range(SLOTS)
    )
    out_ref[...] = (weighted / denominator).astype(out_ref.dtype)
    lse_ref[...] = as_lane_row(row_max + jnp.log(denominator))


def backward_kernel(
    count_ref, q_ref, k_ref, v_ref, grad_ref, att_ref, lse_ref, dq_ref, dk_ref, dv_ref
):
    @pl.when(pl.program_id(0) == 0)
    def _():
        dk_ref[...] = jnp.zeros_like(dk_ref)
        dv_ref[...] = jnp.zeros_like(dv_ref)

    query_head = q_ref[...]
    grad_head = grad_ref[...]
    log_total = lse_ref[...]
    row_delta = as_lane_row(
        jnp.sum(grad_head.astype(jnp.float32) * att_ref[...].astype(jnp.float32), axis=1, keepdims=True)
    )
    query_grad = jnp.zeros(dq_ref.shape, jnp.float32)
    for slot in range(SLOTS):
        mate_keys = k_ref[slot]
        back_probs = jnp.exp(
            slot_scores(mate_keys, query_head) - slot_offset(count_ref, slot, log_total, jnp.inf)
        )
        dv_ref[slot] += jnp.dot(
            back_probs.astype(jnp.bfloat16), grad_head, preferred_element_type=jnp.float32
        )
        prob_grad = lax.dot_general(
            v_ref[slot], grad_head, TRANS_B, preferred_element_type=jnp.float32
        )
        score_grad = (back_probs * (prob_grad - row_delta)).astype(jnp.bfloat16)
        dk_ref[slot] += SCORE_SCALE * jnp.dot(
            score_grad, query_head, preferred_element_type=jnp.float32
        )
        query_grad = query_grad + lax.dot_general(
            score_grad, mate_keys, TRANS_A, preferred_element_type=jnp.float32
        )
    dq_ref[...] = (SCORE_SCALE * query_grad).astype(dq_ref.dtype)


def attention_forward(count, queries, mate_keys, mate_values):
    seq_len, width = queries.shape
    heads = width // HD
    head_block = pl.BlockSpec((seq_len, HD), lambda h, c: (0, h))
    slot_block = pl.BlockSpec((SLOTS, seq_len, HD), lambda h, c: (0, 0, 0))
    return pl.pallas_call(
        forward_kernel,
        grid_spec=pltpu.PrefetchScalarGridSpec(
            num_scalar_prefetch=1,
            grid=(heads,),
            in_specs=[head_block, slot_block, slot_block],
            out_specs=[head_block, pl.BlockSpec((None, 1, seq_len), lambda h, c: (h, 0, 0))],
        ),
        out_shape=[
            jax.ShapeDtypeStruct((seq_len, width), jnp.bfloat16),
            jax.ShapeDtypeStruct((heads, 1, seq_len), jnp.float32),
        ],
    )(count, queries, mate_keys, mate_values)


def attention_backward(count, queries, mate_keys, mate_values, attention_grad, attention, log_rows):
    seq_len, width = queries.shape
    heads = width // HD
    head_block = pl.BlockSpec((seq_len, HD), lambda h, c: (0, h))
    row_block = pl.BlockSpec((None, 1, seq_len), lambda h, c: (h, 0, 0))
    slot_block = pl.BlockSpec((SLOTS, seq_len, HD), lambda h, c: (0, 0, 0))
    return pl.pallas_call(
        backward_kernel,
        grid_spec=pltpu.PrefetchScalarGridSpec(
            num_scalar_prefetch=1,
            grid=(heads,),
            in_specs=[head_block, slot_block, slot_block, head_block, head_block, row_block],
            out_specs=[head_block, slot_block, slot_block],
        ),
        out_shape=[
            jax.ShapeDtypeStruct((seq_len, width), jnp.bfloat16),
            jax.ShapeDtypeStruct((SLOTS, seq_len, HD), jnp.float32),
            jax.ShapeDtypeStruct((SLOTS, seq_len, HD), jnp.float32),
        ],
        compiler_params=pltpu.CompilerParams(dimension_semantics=("arbitrary",)),
    )(count, queries, mate_keys, mate_values, attention_grad, attention, log_rows)


def exchange(block, axis, bit):
    route = [(low, low ^ (1 << bit)) for low in range(lax.axis_size(axis))]
    return lax.ppermute(block, axis, route)


def bit_reversed(distance):
    return ((distance & 1) << 2) | (distance & 2) | ((distance >> 2) & 1)


def ring_route(move):
    route = []
    for low in range(lax.axis_size("resp")):
        place = low % GROUP
        chip, core = divmod(place, 2)
        to_chip, to_core = move(chip, core)
        route.append((low, low - place + (to_chip % (GROUP // 2)) * 2 + to_core))
    return route


RING_ROWS = (0, 1, 3, 5, 6, 7, 2, 4)


def ring_row(partner, my_index):
    chip_step = ((partner >> 1) - (my_index >> 1)) % (GROUP // 2)
    return jnp.asarray(RING_ROWS, jnp.int32)[chip_step * 2 + ((partner ^ my_index) & 1)]


def gather_group(block, my_index):
    from_minus = lax.ppermute(block, "resp", ring_route(lambda x, c: (x + 1, c)))
    from_plus = lax.ppermute(block, "resp", ring_route(lambda x, c: (x - 1, c)))
    from_core = lax.ppermute(block, "resp", ring_route(lambda x, c: (x, 1 - c)))
    relay = jnp.where(my_index % 2 == 0, from_plus, from_minus)
    far = lax.ppermute(relay, "resp", ring_route(lambda x, c: (x - 1, c) if c == 0 else (x + 1, c)))
    core_sides = lax.ppermute(
        jnp.concatenate([from_minus, from_plus], 0), "resp", ring_route(lambda x, c: (x, 1 - c))
    )
    far_other = lax.ppermute(far, "resp", ring_route(lambda x, c: (x, 1 - c)))
    return jnp.concatenate(
        [block, from_core, from_minus, from_plus, core_sides, far, far_other], 0
    )


def return_group(terms):
    for bit in range(GROUP.bit_length() - 1):
        half = terms.shape[0] // 2
        sent = terms[half:].astype(jnp.bfloat16)
        terms = terms[:half] + exchange(sent, "resp", bit).astype(jnp.float32)
    return terms


def head_sum(row_part):
    for bit in range(lax.axis_size("head").bit_length() - 1):
        row_part = row_part + exchange(row_part, "head", bit)
    return row_part


def body(queries, key_states, value_states, partners, counts, norm_gain, out_grad):
    my_index = lax.axis_index("resp")
    seq_len = queries.shape[1]
    mate_rows = bit_reversed(jnp.bitwise_xor(partners[0], my_index))
    count = counts.astype(jnp.int32)
    ring_rows = ring_row(partners[0], my_index)
    mate_keys = jnp.take(gather_group(key_states, my_index), ring_rows, axis=0)
    mate_values = jnp.take(gather_group(value_states, my_index), ring_rows, axis=0)

    attention, log_total = attention_forward(count, queries[0], mate_keys, mate_values)
    attention_flat = attention.astype(jnp.float32)
    scaled_grad = out_grad[0].astype(jnp.float32) * norm_gain
    row_sums = jnp.stack(
        [jnp.sum(attention_flat * attention_flat, -1), jnp.sum(attention_flat * scaled_grad, -1)]
    )
    row_sums = head_sum(row_sums)
    square_sums, dot_sums = row_sums[0], row_sums[1]
    inverse_rms = lax.rsqrt(square_sums / D + EPSILON)
    normed_out = (attention_flat * inverse_rms[:, None] * norm_gain).astype(jnp.bfloat16)[None]
    attention_grad = (
        inverse_rms[:, None] * scaled_grad
        - attention_flat * (inverse_rms**3 * dot_sums / D)[:, None]
    ).astype(jnp.bfloat16)

    query_grads, key_terms, value_terms = attention_backward(
        count, queries[0], mate_keys, mate_values, attention_grad, attention, log_total
    )
    zero_rows = jnp.zeros((GROUP,) + key_terms.shape[1:], jnp.float32)
    key_total = return_group(zero_rows.at[mate_rows].add(key_terms))
    value_total = return_group(zero_rows.at[mate_rows].add(value_terms))
    return (
        normed_out,
        query_grads[None],
        key_total.astype(jnp.bfloat16),
        value_total.astype(jnp.bfloat16),
    )


def solution(mesh):
    placed = (
        P("resp", None, "head"),
        P("resp", None, "head"),
        P("resp", None, "head"),
        P("resp", None),
        P("resp"),
        P("head"),
        P("resp", None, "head"),
    )
    return jax.shard_map(
        body,
        mesh=mesh,
        in_specs=placed,
        out_specs=(
            P("resp", None, "head"),
            P("resp", None, "head"),
            P("resp", None, "head"),
            P("resp", None, "head"),
        ),
        check_vma=False,
    )
```

```python
import functools

import jax
import jax.numpy as jnp
from jax import lax
from jax.experimental import pallas as pl
from jax.experimental.pallas import tpu as pltpu
from jax.sharding import PartitionSpec as P

HD = 128
D = 8192
GROUP = 8
SLOTS = 3


EPSILON = 1e-05
SCORE_SCALE = HD ** (-0.5)

TRANS_B = (((1,), (1,)), ((), ()))
TRANS_A = (((0,), (0,)), ((), ()))


def slot_scores(query_head, mate_keys):
    scores = lax.dot_general(query_head, mate_keys, TRANS_B, preferred_element_type=jnp.float32)
    return scores * SCORE_SCALE


def slot_offset(count_ref, slot, offset, dead):
    return jnp.where(slot < count_ref[0], offset, dead)


def as_lane_row(column):
    return jnp.transpose(jnp.broadcast_to(column, (column.shape[0], HD)))[:1]


def forward_kernel(count_ref, q_ref, k_ref, v_ref, out_ref, lse_ref):
    query_head = q_ref[...]
    scores = [slot_scores(query_head, k_ref[slot]) for slot in range(SLOTS)]
    row_max = functools.reduce(
        jnp.maximum,
        [
            slot_offset(count_ref, slot, jnp.max(block, axis=1, keepdims=True), -jnp.inf)
            for slot, block in enumerate(scores)
        ],
    )
    exps = [
        jnp.exp(block - slot_offset(count_ref, slot, row_max, jnp.inf))
        for slot, block in enumerate(scores)
    ]
    denominator = sum(jnp.sum(block, axis=1, keepdims=True) for block in exps)
    weighted = sum(
        jnp.dot(exps[slot].astype(jnp.bfloat16), v_ref[slot], preferred_element_type=jnp.float32)
        for slot in range(SLOTS)
    )
    out_ref[...] = (weighted / denominator).astype(out_ref.dtype)
    lse_ref[...] = as_lane_row(row_max + jnp.log(denominator))


def backward_kernel(
    count_ref, q_ref, k_ref, v_ref, grad_ref, att_ref, lse_ref, dq_ref, dk_ref, dv_ref
):
    @pl.when(pl.program_id(0) == 0)
    def _():
        dk_ref[...] = jnp.zeros_like(dk_ref)
        dv_ref[...] = jnp.zeros_like(dv_ref)

    query_head = q_ref[...]
    grad_head = grad_ref[...]
    log_total = lse_ref[...]
    row_delta = as_lane_row(
        jnp.sum(grad_head.astype(jnp.float32) * att_ref[...].astype(jnp.float32), axis=1, keepdims=True)
    )
    query_grad = jnp.zeros(dq_ref.shape, jnp.float32)
    for slot in range(SLOTS):
        mate_keys = k_ref[slot]
        back_probs = jnp.exp(
            slot_scores(mate_keys, query_head) - slot_offset(count_ref, slot, log_total, jnp.inf)
        )
        dv_ref[slot] += jnp.dot(
            back_probs.astype(jnp.bfloat16), grad_head, preferred_element_type=jnp.float32
        )
        prob_grad = lax.dot_general(
            v_ref[slot], grad_head, TRANS_B, preferred_element_type=jnp.float32
        )
        score_grad = (back_probs * (prob_grad - row_delta)).astype(jnp.bfloat16)
        dk_ref[slot] += SCORE_SCALE * jnp.dot(
            score_grad, query_head, preferred_element_type=jnp.float32
        )
        query_grad = query_grad + lax.dot_general(
            score_grad, mate_keys, TRANS_A, preferred_element_type=jnp.float32
        )
    dq_ref[...] = (SCORE_SCALE * query_grad).astype(dq_ref.dtype)


def attention_forward(count, queries, mate_keys, mate_values):
    seq_len, width = queries.shape
    heads = width // HD
    head_block = pl.BlockSpec((seq_len, HD), lambda h, c: (0, h))
    slot_block = pl.BlockSpec((SLOTS, seq_len, HD), lambda h, c: (0, 0, 0))
    return pl.pallas_call(
        forward_kernel,
        grid_spec=pltpu.PrefetchScalarGridSpec(
            num_scalar_prefetch=1,
            grid=(heads,),
            in_specs=[head_block, slot_block, slot_block],
            out_specs=[head_block, pl.BlockSpec((None, 1, seq_len), lambda h, c: (h, 0, 0))],
        ),
        out_shape=[
            jax.ShapeDtypeStruct((seq_len, width), jnp.bfloat16),
            jax.ShapeDtypeStruct((heads, 1, seq_len), jnp.float32),
        ],
    )(count, queries, mate_keys, mate_values)


def attention_backward(count, queries, mate_keys, mate_values, attention_grad, attention, log_rows):
    seq_len, width = queries.shape
    heads = width // HD
    head_block = pl.BlockSpec((seq_len, HD), lambda h, c: (0, h))
    row_block = pl.BlockSpec((None, 1, seq_len), lambda h, c: (h, 0, 0))
    slot_block = pl.BlockSpec((SLOTS, seq_len, HD), lambda h, c: (0, 0, 0))
    return pl.pallas_call(
        backward_kernel,
        grid_spec=pltpu.PrefetchScalarGridSpec(
            num_scalar_prefetch=1,
            grid=(heads,),
            in_specs=[head_block, slot_block, slot_block, head_block, head_block, row_block],
            out_specs=[head_block, slot_block, slot_block],
        ),
        out_shape=[
            jax.ShapeDtypeStruct((seq_len, width), jnp.bfloat16),
            jax.ShapeDtypeStruct((SLOTS, seq_len, HD), jnp.float32),
            jax.ShapeDtypeStruct((SLOTS, seq_len, HD), jnp.float32),
        ],
        compiler_params=pltpu.CompilerParams(dimension_semantics=("arbitrary",)),
    )(count, queries, mate_keys, mate_values, attention_grad, attention, log_rows)


def exchange(block, axis, bit):
    route = [(low, low ^ (1 << bit)) for low in range(lax.axis_size(axis))]
    return lax.ppermute(block, axis, route)


def ring_route(move):
    route = []
    for low in range(lax.axis_size("resp")):
        place = low % GROUP
        chip, core = divmod(place, 2)
        to_chip, to_core = move(chip, core)
        route.append((low, low - place + (to_chip % (GROUP // 2)) * 2 + to_core))
    return route


RING_ROWS = (0, 1, 3, 5, 6, 7, 2, 4)


def ring_row(partner, my_index):
    chip_step = ((partner >> 1) - (my_index >> 1)) % (GROUP // 2)
    return jnp.asarray(RING_ROWS, jnp.int32)[chip_step * 2 + ((partner ^ my_index) & 1)]


def gather_group(block, my_index):
    from_minus = lax.ppermute(block, "resp", ring_route(lambda x, c: (x + 1, c)))
    from_plus = lax.ppermute(block, "resp", ring_route(lambda x, c: (x - 1, c)))
    from_core = lax.ppermute(block, "resp", ring_route(lambda x, c: (x, 1 - c)))
    relay = jnp.where(my_index % 2 == 0, from_plus, from_minus)
    far = lax.ppermute(relay, "resp", ring_route(lambda x, c: (x - 1, c) if c == 0 else (x + 1, c)))
    core_sides = lax.ppermute(
        jnp.concatenate([from_minus, from_plus], 0), "resp", ring_route(lambda x, c: (x, 1 - c))
    )
    far_other = lax.ppermute(far, "resp", ring_route(lambda x, c: (x, 1 - c)))
    return jnp.concatenate(
        [block, from_core, from_minus, from_plus, core_sides, far, far_other], 0
    )


def return_group(terms, my_index):
    def send(block, move):
        return lax.ppermute(block.astype(jnp.bfloat16), "resp", ring_route(move)).astype(jnp.float32)

    from_core = send(terms[jnp.array([1, 4, 5, 7])], lambda x, c: (x, 1 - c))
    own = terms[0] + from_core[0]
    minus = terms[2] + from_core[1]
    plus = terms[3] + from_core[2]
    far = terms[6] + from_core[3]
    far_back = send(far, lambda x, c: (x + 1, c) if c == 0 else (x - 1, c))
    is_core0 = my_index % 2 == 0
    plus = plus + jnp.where(is_core0, far_back, 0.0)
    minus = minus + jnp.where(is_core0, 0.0, far_back)
    return own + send(minus, lambda x, c: (x - 1, c)) + send(plus, lambda x, c: (x + 1, c))


def head_sum(row_part):
    for bit in range(lax.axis_size("head").bit_length() - 1):
        row_part = row_part + exchange(row_part, "head", bit)
    return row_part


def body(queries, key_states, value_states, partners, counts, norm_gain, out_grad):
    my_index = lax.axis_index("resp")
    seq_len = queries.shape[1]
    count = counts.astype(jnp.int32)
    ring_rows = ring_row(partners[0], my_index)
    mate_keys = jnp.take(gather_group(key_states, my_index), ring_rows, axis=0)
    mate_values = jnp.take(gather_group(value_states, my_index), ring_rows, axis=0)

    attention, log_total = attention_forward(count, queries[0], mate_keys, mate_values)
    attention_flat = attention.astype(jnp.float32)
    scaled_grad = out_grad[0].astype(jnp.float32) * norm_gain
    row_sums = jnp.stack(
        [jnp.sum(attention_flat * attention_flat, -1), jnp.sum(attention_flat * scaled_grad, -1)]
    )
    row_sums = head_sum(row_sums)
    square_sums, dot_sums = row_sums[0], row_sums[1]
    inverse_rms = lax.rsqrt(square_sums / D + EPSILON)
    normed_out = (attention_flat * inverse_rms[:, None] * norm_gain).astype(jnp.bfloat16)[None]
    attention_grad = (
        inverse_rms[:, None] * scaled_grad
        - attention_flat * (inverse_rms**3 * dot_sums / D)[:, None]
    ).astype(jnp.bfloat16)

    query_grads, key_terms, value_terms = attention_backward(
        count, queries[0], mate_keys, mate_values, attention_grad, attention, log_total
    )
    zero_rows = jnp.zeros((GROUP,) + key_terms.shape[1:], jnp.float32)
    key_total = return_group(zero_rows.at[ring_rows].add(key_terms), my_index)[None]
    value_total = return_group(zero_rows.at[ring_rows].add(value_terms), my_index)[None]
    return (
        normed_out,
        query_grads[None],
        key_total.astype(jnp.bfloat16),
        value_total.astype(jnp.bfloat16),
    )


def solution(mesh):
    placed = (
        P("resp", None, "head"),
        P("resp", None, "head"),
        P("resp", None, "head"),
        P("resp", None),
        P("resp"),
        P("head"),
        P("resp", None, "head"),
    )
    return jax.shard_map(
        body,
        mesh=mesh,
        in_specs=placed,
        out_specs=(
            P("resp", None, "head"),
            P("resp", None, "head"),
            P("resp", None, "head"),
            P("resp", None, "head"),
        ),
        check_vma=False,
    )
```

```python
import functools

import jax
import jax.numpy as jnp
from jax import lax
from jax.experimental import pallas as pl
from jax.experimental.pallas import tpu as pltpu
from jax.sharding import PartitionSpec as P

HD = 128
D = 8192
GROUP = 8
SLOTS = 3


EPSILON = 1e-05
SCORE_SCALE = HD ** (-0.5)

TRANS_B = (((1,), (1,)), ((), ()))
TRANS_A = (((0,), (0,)), ((), ()))


def slot_scores(query_head, mate_keys):
    scores = lax.dot_general(query_head, mate_keys, TRANS_B, preferred_element_type=jnp.float32)
    return scores * SCORE_SCALE


def slot_offset(count_ref, slot, offset, dead):
    return jnp.where(slot < count_ref[0], offset, dead)


def as_lane_row(column):
    return jnp.transpose(jnp.broadcast_to(column, (column.shape[0], HD)))[:1]


def forward_kernel(count_ref, rows_ref, q_ref, *refs):
    k_ref, v_ref, (out_ref, lse_ref) = refs[:SLOTS], refs[SLOTS : 2 * SLOTS], refs[2 * SLOTS :]
    query_head = q_ref[...]
    scores = [slot_scores(query_head, k_ref[slot][...]) for slot in range(SLOTS)]
    row_max = functools.reduce(
        jnp.maximum,
        [
            slot_offset(count_ref, slot, jnp.max(block, axis=1, keepdims=True), -jnp.inf)
            for slot, block in enumerate(scores)
        ],
    )
    exps = [
        jnp.exp(block - slot_offset(count_ref, slot, row_max, jnp.inf))
        for slot, block in enumerate(scores)
    ]
    denominator = sum(jnp.sum(block, axis=1, keepdims=True) for block in exps)
    weighted = sum(
        jnp.dot(exps[slot].astype(jnp.bfloat16), v_ref[slot][...], preferred_element_type=jnp.float32)
        for slot in range(SLOTS)
    )
    out_ref[...] = (weighted / denominator).astype(out_ref.dtype)
    lse_ref[...] = as_lane_row(row_max + jnp.log(denominator))


def backward_kernel(count_ref, rows_ref, q_ref, *refs):
    k_ref, v_ref = refs[:SLOTS], refs[SLOTS : 2 * SLOTS]
    grad_ref, att_ref, lse_ref, dq_ref, dk_ref, dv_ref = refs[2 * SLOTS :]

    @pl.when(pl.program_id(0) == 0)
    def _():
        dk_ref[...] = jnp.zeros_like(dk_ref)
        dv_ref[...] = jnp.zeros_like(dv_ref)

    query_head = q_ref[...]
    grad_head = grad_ref[...]
    log_total = lse_ref[...]
    row_delta = as_lane_row(
        jnp.sum(grad_head.astype(jnp.float32) * att_ref[...].astype(jnp.float32), axis=1, keepdims=True)
    )
    query_grad = jnp.zeros(dq_ref.shape, jnp.float32)
    for slot in range(SLOTS):
        mate_keys = k_ref[slot][...]
        back_probs = jnp.exp(
            slot_scores(mate_keys, query_head) - slot_offset(count_ref, slot, log_total, jnp.inf)
        )
        dv_ref[slot] += jnp.dot(
            back_probs.astype(jnp.bfloat16), grad_head, preferred_element_type=jnp.float32
        )
        prob_grad = lax.dot_general(
            v_ref[slot][...], grad_head, TRANS_B, preferred_element_type=jnp.float32
        )
        score_grad = (back_probs * (prob_grad - row_delta)).astype(jnp.bfloat16)
        dk_ref[slot] += SCORE_SCALE * jnp.dot(
            score_grad, query_head, preferred_element_type=jnp.float32
        )
        query_grad = query_grad + lax.dot_general(
            score_grad, mate_keys, TRANS_A, preferred_element_type=jnp.float32
        )
    dq_ref[...] = (SCORE_SCALE * query_grad).astype(dq_ref.dtype)


def slot_blocks(seq_len):
    return [
        pl.BlockSpec((None, seq_len, HD), lambda h, c, r, slot=slot: (r[slot], 0, 0))
        for slot in range(SLOTS)
    ]


def attention_forward(count, mate_rows, queries, group_keys, group_values):
    seq_len, width = queries.shape
    heads = width // HD
    head_block = pl.BlockSpec((seq_len, HD), lambda h, c, r: (0, h))
    return pl.pallas_call(
        forward_kernel,
        grid_spec=pltpu.PrefetchScalarGridSpec(
            num_scalar_prefetch=2,
            grid=(heads,),
            in_specs=[head_block] + slot_blocks(seq_len) * 2,
            out_specs=[head_block, pl.BlockSpec((None, 1, seq_len), lambda h, c, r: (h, 0, 0))],
        ),
        out_shape=[
            jax.ShapeDtypeStruct((seq_len, width), jnp.bfloat16),
            jax.ShapeDtypeStruct((heads, 1, seq_len), jnp.float32),
        ],
    )(count, mate_rows, queries, *([group_keys] * SLOTS), *([group_values] * SLOTS))


def attention_backward(
    count, mate_rows, queries, group_keys, group_values, attention_grad, attention, log_rows
):
    seq_len, width = queries.shape
    heads = width // HD
    head_block = pl.BlockSpec((seq_len, HD), lambda h, c, r: (0, h))
    row_block = pl.BlockSpec((None, 1, seq_len), lambda h, c, r: (h, 0, 0))
    slot_block = pl.BlockSpec((SLOTS, seq_len, HD), lambda h, c, r: (0, 0, 0))
    return pl.pallas_call(
        backward_kernel,
        grid_spec=pltpu.PrefetchScalarGridSpec(
            num_scalar_prefetch=2,
            grid=(heads,),
            in_specs=[head_block] + slot_blocks(seq_len) * 2 + [head_block, head_block, row_block],
            out_specs=[head_block, slot_block, slot_block],
        ),
        out_shape=[
            jax.ShapeDtypeStruct((seq_len, width), jnp.bfloat16),
            jax.ShapeDtypeStruct((SLOTS, seq_len, HD), jnp.float32),
            jax.ShapeDtypeStruct((SLOTS, seq_len, HD), jnp.float32),
        ],
        compiler_params=pltpu.CompilerParams(dimension_semantics=("arbitrary",)),
    )(
        count, mate_rows, queries, *([group_keys] * SLOTS), *([group_values] * SLOTS),
        attention_grad, attention, log_rows,
    )


def exchange(block, axis, bit):
    route = [(low, low ^ (1 << bit)) for low in range(lax.axis_size(axis))]
    return lax.ppermute(block, axis, route)


def ring_route(move):
    route = []
    for low in range(lax.axis_size("resp")):
        place = low % GROUP
        chip, core = divmod(place, 2)
        to_chip, to_core = move(chip, core)
        route.append((low, low - place + (to_chip % (GROUP // 2)) * 2 + to_core))
    return route


RING_ROWS = (0, 1, 3, 5, 6, 7, 2, 4)


def ring_row(partner, my_index):
    chip_step = ((partner >> 1) - (my_index >> 1)) % (GROUP // 2)
    return jnp.asarray(RING_ROWS, jnp.int32)[chip_step * 2 + ((partner ^ my_index) & 1)]


def gather_group(block, my_index):
    from_minus = lax.ppermute(block, "resp", ring_route(lambda x, c: (x + 1, c)))
    from_plus = lax.ppermute(block, "resp", ring_route(lambda x, c: (x - 1, c)))
    from_core = lax.ppermute(block, "resp", ring_route(lambda x, c: (x, 1 - c)))
    relay = jnp.where(my_index % 2 == 0, from_plus, from_minus)
    far = lax.ppermute(relay, "resp", ring_route(lambda x, c: (x - 1, c) if c == 0 else (x + 1, c)))
    core_sides = lax.ppermute(
        jnp.concatenate([from_minus, from_plus], 0), "resp", ring_route(lambda x, c: (x, 1 - c))
    )
    far_other = lax.ppermute(far, "resp", ring_route(lambda x, c: (x, 1 - c)))
    return jnp.concatenate(
        [block, from_core, from_minus, from_plus, core_sides, far, far_other], 0
    )


def return_group(terms, my_index):
    def send(block, move):
        return lax.ppermute(block.astype(jnp.bfloat16), "resp", ring_route(move)).astype(jnp.float32)

    from_core = send(terms[jnp.array([1, 4, 5, 7])], lambda x, c: (x, 1 - c))
    own = terms[0] + from_core[0]
    minus = terms[2] + from_core[1]
    plus = terms[3] + from_core[2]
    far = terms[6] + from_core[3]
    far_back = send(far, lambda x, c: (x + 1, c) if c == 0 else (x - 1, c))
    is_core0 = my_index % 2 == 0
    plus = plus + jnp.where(is_core0, far_back, 0.0)
    minus = minus + jnp.where(is_core0, 0.0, far_back)
    return own + send(minus, lambda x, c: (x - 1, c)) + send(plus, lambda x, c: (x + 1, c))


def head_sum(row_part):
    for bit in range(lax.axis_size("head").bit_length() - 1):
        row_part = row_part + exchange(row_part, "head", bit)
    return row_part


def body(queries, key_states, value_states, partners, counts, norm_gain, out_grad):
    my_index = lax.axis_index("resp")
    seq_len = queries.shape[1]
    count = counts.astype(jnp.int32)
    ring_rows = ring_row(partners[0], my_index)
    group_keys = gather_group(key_states, my_index)
    group_values = gather_group(value_states, my_index)

    attention, log_total = attention_forward(count, ring_rows, queries[0], group_keys, group_values)
    attention_flat = attention.astype(jnp.float32)
    scaled_grad = out_grad[0].astype(jnp.float32) * norm_gain
    row_sums = jnp.stack(
        [jnp.sum(attention_flat * attention_flat, -1), jnp.sum(attention_flat * scaled_grad, -1)]
    )
    row_sums = head_sum(row_sums)
    square_sums, dot_sums = row_sums[0], row_sums[1]
    inverse_rms = lax.rsqrt(square_sums / D + EPSILON)
    normed_out = (attention_flat * inverse_rms[:, None] * norm_gain).astype(jnp.bfloat16)[None]
    attention_grad = (
        inverse_rms[:, None] * scaled_grad
        - attention_flat * (inverse_rms**3 * dot_sums / D)[:, None]
    ).astype(jnp.bfloat16)

    query_grads, key_terms, value_terms = attention_backward(
        count, ring_rows, queries[0], group_keys, group_values, attention_grad, attention, log_total
    )
    zero_rows = jnp.zeros((GROUP,) + key_terms.shape[1:], jnp.float32)
    key_total = return_group(zero_rows.at[ring_rows].add(key_terms), my_index)[None]
    value_total = return_group(zero_rows.at[ring_rows].add(value_terms), my_index)[None]
    return (
        normed_out,
        query_grads[None],
        key_total.astype(jnp.bfloat16),
        value_total.astype(jnp.bfloat16),
    )


def solution(mesh):
    placed = (
        P("resp", None, "head"),
        P("resp", None, "head"),
        P("resp", None, "head"),
        P("resp", None),
        P("resp"),
        P("head"),
        P("resp", None, "head"),
    )
    return jax.shard_map(
        body,
        mesh=mesh,
        in_specs=placed,
        out_specs=(
            P("resp", None, "head"),
            P("resp", None, "head"),
            P("resp", None, "head"),
            P("resp", None, "head"),
        ),
        check_vma=False,
    )
```

```python
import functools

import jax
import jax.numpy as jnp
from jax import lax
from jax.experimental import pallas as pl
from jax.experimental.pallas import tpu as pltpu
from jax.sharding import PartitionSpec as P

HD = 128
D = 8192
GROUP = 8
SLOTS = 3


EPSILON = 1e-05
SCORE_SCALE = HD ** (-0.5)

TRANS_B = (((1,), (1,)), ((), ()))
TRANS_A = (((0,), (0,)), ((), ()))


def slot_scores(query_head, mate_keys):
    scores = lax.dot_general(query_head, mate_keys, TRANS_B, preferred_element_type=jnp.float32)
    return scores * SCORE_SCALE


def slot_offset(count_ref, slot, offset, dead):
    return jnp.where(slot < count_ref[0], offset, dead)


def as_lane_row(column):
    return jnp.transpose(jnp.broadcast_to(column, (column.shape[0], HD)))[:1]


def forward_kernel(count_ref, rows_ref, q_ref, *refs):
    k_ref, v_ref, (out_ref, lse_ref) = refs[:SLOTS], refs[SLOTS : 2 * SLOTS], refs[2 * SLOTS :]
    query_head = q_ref[...]
    scores = [slot_scores(query_head, k_ref[slot][...]) for slot in range(SLOTS)]
    row_max = functools.reduce(
        jnp.maximum,
        [
            slot_offset(count_ref, slot, jnp.max(block, axis=1, keepdims=True), -jnp.inf)
            for slot, block in enumerate(scores)
        ],
    )
    exps = [
        jnp.exp(block - slot_offset(count_ref, slot, row_max, jnp.inf))
        for slot, block in enumerate(scores)
    ]
    denominator = sum(jnp.sum(block, axis=1, keepdims=True) for block in exps)
    weighted = sum(
        jnp.dot(exps[slot].astype(jnp.bfloat16), v_ref[slot][...], preferred_element_type=jnp.float32)
        for slot in range(SLOTS)
    )
    out_ref[...] = (weighted / denominator).astype(out_ref.dtype)
    lse_ref[...] = as_lane_row(row_max + jnp.log(denominator))


def backward_kernel(count_ref, rows_ref, q_ref, *refs):
    k_ref, v_ref = refs[:SLOTS], refs[SLOTS : 2 * SLOTS]
    grad_ref, att_ref, lse_ref, dq_ref, dk_ref, dv_ref = refs[2 * SLOTS :]

    @pl.when(pl.program_id(0) == 0)
    def _():
        dk_ref[...] = jnp.zeros_like(dk_ref)
        dv_ref[...] = jnp.zeros_like(dv_ref)

    query_head = q_ref[...]
    grad_head = grad_ref[...]
    log_total = lse_ref[...]
    row_delta = as_lane_row(
        jnp.sum(grad_head.astype(jnp.float32) * att_ref[...].astype(jnp.float32), axis=1, keepdims=True)
    )
    query_grad = jnp.zeros(dq_ref.shape, jnp.float32)
    for slot in range(SLOTS):
        mate_keys = k_ref[slot][...]
        back_probs = jnp.exp(
            slot_scores(mate_keys, query_head) - slot_offset(count_ref, slot, log_total, jnp.inf)
        )
        dv_ref[slot] += jnp.dot(
            back_probs.astype(jnp.bfloat16), grad_head, preferred_element_type=jnp.float32
        )
        prob_grad = lax.dot_general(
            v_ref[slot][...], grad_head, TRANS_B, preferred_element_type=jnp.float32
        )
        score_grad = (back_probs * (prob_grad - row_delta)).astype(jnp.bfloat16)
        dk_ref[slot] += SCORE_SCALE * jnp.dot(
            score_grad, query_head, preferred_element_type=jnp.float32
        )
        query_grad = query_grad + lax.dot_general(
            score_grad, mate_keys, TRANS_A, preferred_element_type=jnp.float32
        )
    dq_ref[...] = (SCORE_SCALE * query_grad).astype(dq_ref.dtype)


def slot_blocks(seq_len):
    return [
        pl.BlockSpec((None, seq_len, HD), lambda h, c, r, slot=slot: (r[slot], 0, 0))
        for slot in range(SLOTS)
    ]


def attention_forward(count, mate_rows, queries, group_keys, group_values):
    seq_len, width = queries.shape
    heads = width // HD
    head_block = pl.BlockSpec((seq_len, HD), lambda h, c, r: (0, h))
    return pl.pallas_call(
        forward_kernel,
        grid_spec=pltpu.PrefetchScalarGridSpec(
            num_scalar_prefetch=2,
            grid=(heads,),
            in_specs=[head_block] + slot_blocks(seq_len) * 2,
            out_specs=[head_block, pl.BlockSpec((None, 1, seq_len), lambda h, c, r: (h, 0, 0))],
        ),
        out_shape=[
            jax.ShapeDtypeStruct((seq_len, width), jnp.bfloat16),
            jax.ShapeDtypeStruct((heads, 1, seq_len), jnp.float32),
        ],
    )(count, mate_rows, queries, *([group_keys] * SLOTS), *([group_values] * SLOTS))


def attention_backward(
    count, mate_rows, queries, group_keys, group_values, attention_grad, attention, log_rows
):
    seq_len, width = queries.shape
    heads = width // HD
    head_block = pl.BlockSpec((seq_len, HD), lambda h, c, r: (0, h))
    row_block = pl.BlockSpec((None, 1, seq_len), lambda h, c, r: (h, 0, 0))
    slot_block = pl.BlockSpec((SLOTS, seq_len, HD), lambda h, c, r: (0, 0, 0))
    return pl.pallas_call(
        backward_kernel,
        grid_spec=pltpu.PrefetchScalarGridSpec(
            num_scalar_prefetch=2,
            grid=(heads,),
            in_specs=[head_block] + slot_blocks(seq_len) * 2 + [head_block, head_block, row_block],
            out_specs=[head_block, slot_block, slot_block],
        ),
        out_shape=[
            jax.ShapeDtypeStruct((seq_len, width), jnp.bfloat16),
            jax.ShapeDtypeStruct((SLOTS, seq_len, HD), jnp.float32),
            jax.ShapeDtypeStruct((SLOTS, seq_len, HD), jnp.float32),
        ],
        compiler_params=pltpu.CompilerParams(dimension_semantics=("arbitrary",)),
    )(
        count, mate_rows, queries, *([group_keys] * SLOTS), *([group_values] * SLOTS),
        attention_grad, attention, log_rows,
    )


def exchange(block, axis, bit):
    route = [(low, low ^ (1 << bit)) for low in range(lax.axis_size(axis))]
    return lax.ppermute(block, axis, route)


def ring_route(move):
    route = []
    for low in range(lax.axis_size("resp")):
        place = low % GROUP
        chip, core = divmod(place, 2)
        to_chip, to_core = move(chip, core)
        route.append((low, low - place + (to_chip % (GROUP // 2)) * 2 + to_core))
    return route


CHIP_STEP_ROWS = (0, 2, 3, 1)


def ring_row(partner, my_index):
    chip_step = ((partner >> 1) - (my_index >> 1)) % (GROUP // 2)
    other_core = (partner ^ my_index) & 1
    return other_core * 4 + jnp.asarray(CHIP_STEP_ROWS, jnp.int32)[chip_step]


def gather_group(block, my_index):
    from_minus = lax.ppermute(block, "resp", ring_route(lambda x, c: (x + 1, c)))
    from_plus = lax.ppermute(block, "resp", ring_route(lambda x, c: (x - 1, c)))
    from_core = lax.ppermute(block, "resp", ring_route(lambda x, c: (x, 1 - c)))
    relay = jnp.where(my_index % 2 == 0, from_plus, from_minus)
    far = lax.ppermute(relay, "resp", ring_route(lambda x, c: (x - 1, c) if c == 0 else (x + 1, c)))
    core_sides = lax.ppermute(
        jnp.concatenate([from_minus, from_plus], 0), "resp", ring_route(lambda x, c: (x, 1 - c))
    )
    far_other = lax.ppermute(far, "resp", ring_route(lambda x, c: (x, 1 - c)))
    return jnp.concatenate(
        [block, from_minus, from_plus, far, from_core, core_sides, far_other], 0
    )


def return_group(terms, my_index):
    def send(block, move):
        return lax.ppermute(block.astype(jnp.bfloat16), "resp", ring_route(move)).astype(jnp.float32)

    kept = terms[:4] + send(terms[4:], lambda x, c: (x, 1 - c))
    own, minus, plus, far = kept[0], kept[1], kept[2], kept[3]
    far_back = send(far, lambda x, c: (x + 1, c) if c == 0 else (x - 1, c))
    is_core0 = my_index % 2 == 0
    plus = plus + jnp.where(is_core0, far_back, 0.0)
    minus = minus + jnp.where(is_core0, 0.0, far_back)
    return own + send(minus, lambda x, c: (x - 1, c)) + send(plus, lambda x, c: (x + 1, c))


def head_sum(row_part):
    for bit in range(lax.axis_size("head").bit_length() - 1):
        row_part = row_part + exchange(row_part, "head", bit)
    return row_part


def body(queries, key_states, value_states, partners, counts, norm_gain, out_grad):
    my_index = lax.axis_index("resp")
    seq_len = queries.shape[1]
    count = counts.astype(jnp.int32)
    ring_rows = ring_row(partners[0], my_index)
    group_keys = gather_group(key_states, my_index)
    group_values = gather_group(value_states, my_index)

    attention, log_total = attention_forward(count, ring_rows, queries[0], group_keys, group_values)
    attention_flat = attention.astype(jnp.float32)
    scaled_grad = out_grad[0].astype(jnp.float32) * norm_gain
    row_sums = jnp.stack(
        [jnp.sum(attention_flat * attention_flat, -1), jnp.sum(attention_flat * scaled_grad, -1)]
    )
    row_sums = head_sum(row_sums)
    square_sums, dot_sums = row_sums[0], row_sums[1]
    inverse_rms = lax.rsqrt(square_sums / D + EPSILON)
    normed_out = (attention_flat * inverse_rms[:, None] * norm_gain).astype(jnp.bfloat16)[None]
    attention_grad = (
        inverse_rms[:, None] * scaled_grad
        - attention_flat * (inverse_rms**3 * dot_sums / D)[:, None]
    ).astype(jnp.bfloat16)

    query_grads, key_terms, value_terms = attention_backward(
        count, ring_rows, queries[0], group_keys, group_values, attention_grad, attention, log_total
    )
    zero_rows = jnp.zeros((GROUP,) + key_terms.shape[1:], jnp.float32)
    key_total = return_group(zero_rows.at[ring_rows].add(key_terms), my_index)[None]
    value_total = return_group(zero_rows.at[ring_rows].add(value_terms), my_index)[None]
    return (
        normed_out,
        query_grads[None],
        key_total.astype(jnp.bfloat16),
        value_total.astype(jnp.bfloat16),
    )


def solution(mesh):
    placed = (
        P("resp", None, "head"),
        P("resp", None, "head"),
        P("resp", None, "head"),
        P("resp", None),
        P("resp"),
        P("head"),
        P("resp", None, "head"),
    )
    return jax.shard_map(
        body,
        mesh=mesh,
        in_specs=placed,
        out_specs=(
            P("resp", None, "head"),
            P("resp", None, "head"),
            P("resp", None, "head"),
            P("resp", None, "head"),
        ),
        check_vma=False,
    )
```

```python
import functools

import jax
import jax.numpy as jnp
from jax import lax
from jax.experimental import pallas as pl
from jax.experimental.pallas import tpu as pltpu
from jax.sharding import PartitionSpec as P

HD = 128
D = 8192
GROUP = 8
SLOTS = 3


EPSILON = 1e-05
SCORE_SCALE = HD ** (-0.5)

TRANS_B = (((1,), (1,)), ((), ()))
TRANS_A = (((0,), (0,)), ((), ()))


def slot_scores(query_head, mate_keys):
    scores = lax.dot_general(query_head, mate_keys, TRANS_B, preferred_element_type=jnp.float32)
    return scores * SCORE_SCALE


def slot_offset(count_ref, slot, offset, dead):
    return jnp.where(slot < count_ref[0], offset, dead)


def as_lane_row(column):
    return jnp.transpose(jnp.broadcast_to(column, (column.shape[0], HD)))[:1]


def forward_kernel(count_ref, rows_ref, q_ref, *refs):
    k_ref, v_ref, (out_ref, lse_ref) = refs[:SLOTS], refs[SLOTS : 2 * SLOTS], refs[2 * SLOTS :]
    query_head = q_ref[...]
    scores = [slot_scores(query_head, k_ref[slot][...]) for slot in range(SLOTS)]
    row_max = functools.reduce(
        jnp.maximum,
        [
            slot_offset(count_ref, slot, jnp.max(block, axis=1, keepdims=True), -jnp.inf)
            for slot, block in enumerate(scores)
        ],
    )
    exps = [
        jnp.exp(block - slot_offset(count_ref, slot, row_max, jnp.inf))
        for slot, block in enumerate(scores)
    ]
    denominator = sum(jnp.sum(block, axis=1, keepdims=True) for block in exps)
    weighted = sum(
        jnp.dot(exps[slot].astype(jnp.bfloat16), v_ref[slot][...], preferred_element_type=jnp.float32)
        for slot in range(SLOTS)
    )
    out_ref[...] = (weighted / denominator).astype(out_ref.dtype)
    lse_ref[...] = as_lane_row(row_max + jnp.log(denominator))


def backward_kernel(count_ref, rows_ref, q_ref, *refs):
    k_ref, v_ref = refs[:SLOTS], refs[SLOTS : 2 * SLOTS]
    grad_ref, att_ref, lse_ref, dq_ref, dk_ref, dv_ref = refs[2 * SLOTS :]

    @pl.when(pl.program_id(0) == 0)
    def _():
        dk_ref[...] = jnp.zeros_like(dk_ref)
        dv_ref[...] = jnp.zeros_like(dv_ref)

    query_head = q_ref[...]
    grad_head = grad_ref[...]
    log_total = lse_ref[...]
    row_delta = as_lane_row(
        jnp.sum(grad_head.astype(jnp.float32) * att_ref[...].astype(jnp.float32), axis=1, keepdims=True)
    )
    query_grad = jnp.zeros(dq_ref.shape, jnp.float32)
    for slot in range(SLOTS):
        mate_keys = k_ref[slot][...]
        back_probs = jnp.exp(
            slot_scores(mate_keys, query_head) - slot_offset(count_ref, slot, log_total, jnp.inf)
        )
        dv_ref[slot] += jnp.dot(
            back_probs.astype(jnp.bfloat16), grad_head, preferred_element_type=jnp.float32
        )
        prob_grad = lax.dot_general(
            v_ref[slot][...], grad_head, TRANS_B, preferred_element_type=jnp.float32
        )
        score_grad = (back_probs * (prob_grad - row_delta)).astype(jnp.bfloat16)
        dk_ref[slot] += SCORE_SCALE * jnp.dot(
            score_grad, query_head, preferred_element_type=jnp.float32
        )
        query_grad = query_grad + lax.dot_general(
            score_grad, mate_keys, TRANS_A, preferred_element_type=jnp.float32
        )
    dq_ref[...] = (SCORE_SCALE * query_grad).astype(dq_ref.dtype)


def slot_blocks(seq_len):
    return [
        pl.BlockSpec((None, seq_len, HD), lambda h, c, r, slot=slot: (r[slot], 0, 0))
        for slot in range(SLOTS)
    ]


def attention_forward(count, mate_rows, queries, group_keys, group_values):
    seq_len, width = queries.shape
    heads = width // HD
    head_block = pl.BlockSpec((seq_len, HD), lambda h, c, r: (0, h))
    return pl.pallas_call(
        forward_kernel,
        grid_spec=pltpu.PrefetchScalarGridSpec(
            num_scalar_prefetch=2,
            grid=(heads,),
            in_specs=[head_block] + slot_blocks(seq_len) * 2,
            out_specs=[head_block, pl.BlockSpec((None, 1, seq_len), lambda h, c, r: (h, 0, 0))],
        ),
        out_shape=[
            jax.ShapeDtypeStruct((seq_len, width), jnp.bfloat16),
            jax.ShapeDtypeStruct((heads, 1, seq_len), jnp.float32),
        ],
    )(count, mate_rows, queries, *([group_keys] * SLOTS), *([group_values] * SLOTS))


def attention_backward(
    count, mate_rows, queries, group_keys, group_values, attention_grad, attention, log_rows
):
    seq_len, width = queries.shape
    heads = width // HD
    head_block = pl.BlockSpec((seq_len, HD), lambda h, c, r: (0, h))
    row_block = pl.BlockSpec((None, 1, seq_len), lambda h, c, r: (h, 0, 0))
    slot_block = pl.BlockSpec((SLOTS, seq_len, HD), lambda h, c, r: (0, 0, 0))
    return pl.pallas_call(
        backward_kernel,
        grid_spec=pltpu.PrefetchScalarGridSpec(
            num_scalar_prefetch=2,
            grid=(heads,),
            in_specs=[head_block] + slot_blocks(seq_len) * 2 + [head_block, head_block, row_block],
            out_specs=[head_block, slot_block, slot_block],
        ),
        out_shape=[
            jax.ShapeDtypeStruct((seq_len, width), jnp.bfloat16),
            jax.ShapeDtypeStruct((SLOTS, seq_len, HD), jnp.float32),
            jax.ShapeDtypeStruct((SLOTS, seq_len, HD), jnp.float32),
        ],
        compiler_params=pltpu.CompilerParams(dimension_semantics=("arbitrary",)),
    )(
        count, mate_rows, queries, *([group_keys] * SLOTS), *([group_values] * SLOTS),
        attention_grad, attention, log_rows,
    )


def exchange(block, axis, bit):
    route = [(low, low ^ (1 << bit)) for low in range(lax.axis_size(axis))]
    return lax.ppermute(block, axis, route)


def ring_route(move):
    route = []
    for low in range(lax.axis_size("resp")):
        place = low % GROUP
        chip, core = divmod(place, 2)
        to_chip, to_core = move(chip, core)
        route.append((low, low - place + (to_chip % (GROUP // 2)) * 2 + to_core))
    return route


CHIP_STEP_ROWS = (0, 2, 3, 1)


def ring_row(partner, my_index):
    chip_step = ((partner >> 1) - (my_index >> 1)) % (GROUP // 2)
    other_core = (partner ^ my_index) & 1
    return other_core * 4 + jnp.asarray(CHIP_STEP_ROWS, jnp.int32)[chip_step]


def gather_group(block, my_index):
    from_minus = lax.ppermute(block, "resp", ring_route(lambda x, c: (x + 1, c)))
    from_plus = lax.ppermute(block, "resp", ring_route(lambda x, c: (x - 1, c)))
    from_core = lax.ppermute(block, "resp", ring_route(lambda x, c: (x, 1 - c)))
    relay = jnp.where(my_index % 2 == 0, from_plus, from_minus)
    far = lax.ppermute(relay, "resp", ring_route(lambda x, c: (x - 1, c) if c == 0 else (x + 1, c)))
    core_sides = lax.ppermute(
        jnp.concatenate([from_minus, from_plus], 0), "resp", ring_route(lambda x, c: (x, 1 - c))
    )
    far_other = lax.ppermute(far, "resp", ring_route(lambda x, c: (x, 1 - c)))
    return jnp.concatenate(
        [block, from_minus, from_plus, far, from_core, core_sides, far_other], 0
    )


def return_group(terms, my_index):
    def send(block, move):
        return lax.ppermute(block.astype(jnp.bfloat16), "resp", ring_route(move)).astype(jnp.float32)

    kept = terms[:4] + send(terms[4:], lambda x, c: (x, 1 - c))
    own, minus, plus, far = kept[0], kept[1], kept[2], kept[3]
    far_back = send(far, lambda x, c: (x + 1, c) if c == 0 else (x - 1, c))
    is_core0 = my_index % 2 == 0
    plus = plus + jnp.where(is_core0, far_back, 0.0)
    minus = minus + jnp.where(is_core0, 0.0, far_back)
    return own + send(minus, lambda x, c: (x - 1, c)) + send(plus, lambda x, c: (x + 1, c))


def head_sum(row_part):
    heads = lax.axis_size("head")
    quad = row_part
    for distance in range(1, 4):
        quad = quad + lax.ppermute(row_part, "head", [(low, low ^ distance) for low in range(heads)])
    return quad + lax.ppermute(quad, "head", [(low, low ^ 4) for low in range(heads)])


def body(queries, key_states, value_states, partners, counts, norm_gain, out_grad):
    my_index = lax.axis_index("resp")
    seq_len = queries.shape[1]
    count = counts.astype(jnp.int32)
    ring_rows = ring_row(partners[0], my_index)
    group_keys = gather_group(key_states, my_index)
    group_values = gather_group(value_states, my_index)

    attention, log_total = attention_forward(count, ring_rows, queries[0], group_keys, group_values)
    attention_flat = attention.astype(jnp.float32)
    scaled_grad = out_grad[0].astype(jnp.float32) * norm_gain
    row_sums = jnp.stack(
        [jnp.sum(attention_flat * attention_flat, -1), jnp.sum(attention_flat * scaled_grad, -1)]
    )
    row_sums = head_sum(row_sums)
    square_sums, dot_sums = row_sums[0], row_sums[1]
    inverse_rms = lax.rsqrt(square_sums / D + EPSILON)
    normed_out = (attention_flat * inverse_rms[:, None] * norm_gain).astype(jnp.bfloat16)[None]
    attention_grad = (
        inverse_rms[:, None] * scaled_grad
        - attention_flat * (inverse_rms**3 * dot_sums / D)[:, None]
    ).astype(jnp.bfloat16)

    query_grads, key_terms, value_terms = attention_backward(
        count, ring_rows, queries[0], group_keys, group_values, attention_grad, attention, log_total
    )
    zero_rows = jnp.zeros((GROUP,) + key_terms.shape[1:], jnp.float32)
    key_total = return_group(zero_rows.at[ring_rows].add(key_terms), my_index)[None]
    value_total = return_group(zero_rows.at[ring_rows].add(value_terms), my_index)[None]
    return (
        normed_out,
        query_grads[None],
        key_total.astype(jnp.bfloat16),
        value_total.astype(jnp.bfloat16),
    )


def solution(mesh):
    placed = (
        P("resp", None, "head"),
        P("resp", None, "head"),
        P("resp", None, "head"),
        P("resp", None),
        P("resp"),
        P("head"),
        P("resp", None, "head"),
    )
    return jax.shard_map(
        body,
        mesh=mesh,
        in_specs=placed,
        out_specs=(
            P("resp", None, "head"),
            P("resp", None, "head"),
            P("resp", None, "head"),
            P("resp", None, "head"),
        ),
        check_vma=False,
    )
```

```python
import functools

import jax
import jax.numpy as jnp
from jax import lax
from jax.experimental import pallas as pl
from jax.experimental.pallas import tpu as pltpu
from jax.sharding import PartitionSpec as P

HD = 128
D = 8192
GROUP = 8
SLOTS = 3


EPSILON = 1e-05
SCORE_SCALE = HD ** (-0.5)

TRANS_B = (((1,), (1,)), ((), ()))
TRANS_A = (((0,), (0,)), ((), ()))


def slot_scores(query_head, mate_keys):
    scores = lax.dot_general(query_head, mate_keys, TRANS_B, preferred_element_type=jnp.float32)
    return scores * SCORE_SCALE


def slot_offset(count_ref, slot, offset, dead):
    return jnp.where(slot < count_ref[0], offset, dead)


def as_lane_row(column):
    return jnp.transpose(jnp.broadcast_to(column, (column.shape[0], HD)))[:1]


def forward_kernel(count_ref, rows_ref, q_ref, *refs):
    k_ref, v_ref, (out_ref, lse_ref) = refs[:SLOTS], refs[SLOTS : 2 * SLOTS], refs[2 * SLOTS :]
    query_head = q_ref[...]
    scores = [slot_scores(query_head, k_ref[slot][...]) for slot in range(SLOTS)]
    row_max = functools.reduce(
        jnp.maximum,
        [
            slot_offset(count_ref, slot, jnp.max(block, axis=1, keepdims=True), -jnp.inf)
            for slot, block in enumerate(scores)
        ],
    )
    exps = [
        jnp.exp(block - slot_offset(count_ref, slot, row_max, jnp.inf))
        for slot, block in enumerate(scores)
    ]
    denominator = sum(jnp.sum(block, axis=1, keepdims=True) for block in exps)
    weighted = sum(
        jnp.dot(exps[slot].astype(jnp.bfloat16), v_ref[slot][...], preferred_element_type=jnp.float32)
        for slot in range(SLOTS)
    )
    out_ref[...] = (weighted / denominator).astype(out_ref.dtype)
    lse_ref[...] = as_lane_row(row_max + jnp.log(denominator))


def backward_kernel(count_ref, rows_ref, q_ref, *refs):
    k_ref, v_ref = refs[:SLOTS], refs[SLOTS : 2 * SLOTS]
    grad_ref, att_ref, lse_ref, dq_ref, dk_ref, dv_ref = refs[2 * SLOTS :]

    @pl.when(pl.program_id(0) == 0)
    def _():
        dk_ref[...] = jnp.zeros_like(dk_ref)
        dv_ref[...] = jnp.zeros_like(dv_ref)

    query_head = q_ref[...]
    grad_head = grad_ref[...]
    log_total = lse_ref[...]
    row_delta = as_lane_row(
        jnp.sum(grad_head.astype(jnp.float32) * att_ref[...].astype(jnp.float32), axis=1, keepdims=True)
    )
    query_grad = jnp.zeros(dq_ref.shape, jnp.float32)
    for slot in range(SLOTS):
        mate_keys = k_ref[slot][...]
        back_probs = jnp.exp(
            slot_scores(mate_keys, query_head) - slot_offset(count_ref, slot, log_total, jnp.inf)
        )
        dv_ref[slot] += jnp.dot(
            back_probs.astype(jnp.bfloat16), grad_head, preferred_element_type=jnp.float32
        )
        prob_grad = lax.dot_general(
            v_ref[slot][...], grad_head, TRANS_B, preferred_element_type=jnp.float32
        )
        score_grad = (back_probs * (prob_grad - row_delta)).astype(jnp.bfloat16)
        dk_ref[slot] += SCORE_SCALE * jnp.dot(
            score_grad, query_head, preferred_element_type=jnp.float32
        )
        query_grad = query_grad + lax.dot_general(
            score_grad, mate_keys, TRANS_A, preferred_element_type=jnp.float32
        )
    dq_ref[...] = (SCORE_SCALE * query_grad).astype(dq_ref.dtype)


def slot_blocks(seq_len):
    return [
        pl.BlockSpec((None, seq_len, HD), lambda h, c, r, slot=slot: (r[slot], 0, 0))
        for slot in range(SLOTS)
    ]


def attention_forward(count, mate_rows, queries, group_keys, group_values):
    seq_len, width = queries.shape
    heads = width // HD
    head_block = pl.BlockSpec((seq_len, HD), lambda h, c, r: (0, h))
    return pl.pallas_call(
        forward_kernel,
        grid_spec=pltpu.PrefetchScalarGridSpec(
            num_scalar_prefetch=2,
            grid=(heads,),
            in_specs=[head_block] + slot_blocks(seq_len) * 2,
            out_specs=[head_block, pl.BlockSpec((None, 1, seq_len), lambda h, c, r: (h, 0, 0))],
        ),
        out_shape=[
            jax.ShapeDtypeStruct((seq_len, width), jnp.bfloat16),
            jax.ShapeDtypeStruct((heads, 1, seq_len), jnp.float32),
        ],
    )(count, mate_rows, queries, *([group_keys] * SLOTS), *([group_values] * SLOTS))


def attention_backward(
    count, mate_rows, queries, group_keys, group_values, attention_grad, attention, log_rows
):
    seq_len, width = queries.shape
    heads = width // HD
    head_block = pl.BlockSpec((seq_len, HD), lambda h, c, r: (0, h))
    row_block = pl.BlockSpec((None, 1, seq_len), lambda h, c, r: (h, 0, 0))
    slot_block = pl.BlockSpec((SLOTS, seq_len, HD), lambda h, c, r: (0, 0, 0))
    return pl.pallas_call(
        backward_kernel,
        grid_spec=pltpu.PrefetchScalarGridSpec(
            num_scalar_prefetch=2,
            grid=(heads,),
            in_specs=[head_block] + slot_blocks(seq_len) * 2 + [head_block, head_block, row_block],
            out_specs=[head_block, slot_block, slot_block],
        ),
        out_shape=[
            jax.ShapeDtypeStruct((seq_len, width), jnp.bfloat16),
            jax.ShapeDtypeStruct((SLOTS, seq_len, HD), jnp.float32),
            jax.ShapeDtypeStruct((SLOTS, seq_len, HD), jnp.float32),
        ],
        compiler_params=pltpu.CompilerParams(dimension_semantics=("arbitrary",)),
    )(
        count, mate_rows, queries, *([group_keys] * SLOTS), *([group_values] * SLOTS),
        attention_grad, attention, log_rows,
    )


def exchange(block, axis, bit):
    route = [(low, low ^ (1 << bit)) for low in range(lax.axis_size(axis))]
    return lax.ppermute(block, axis, route)


def ring_route(move):
    route = []
    for low in range(lax.axis_size("resp")):
        place = low % GROUP
        chip, core = divmod(place, 2)
        to_chip, to_core = move(chip, core)
        route.append((low, low - place + (to_chip % (GROUP // 2)) * 2 + to_core))
    return route


def ring_row(partner, my_index):
    chip_step = ((partner >> 1) - (my_index >> 1)) % (GROUP // 2)
    other_core = (partner ^ my_index) & 1
    step_row = jnp.where(chip_step == 1, 2, jnp.where(chip_step == 2, 3, jnp.where(chip_step == 3, 1, 0)))
    return other_core * 4 + step_row


def gather_group(block, my_index):
    from_minus = lax.ppermute(block, "resp", ring_route(lambda x, c: (x + 1, c)))
    from_plus = lax.ppermute(block, "resp", ring_route(lambda x, c: (x - 1, c)))
    from_core = lax.ppermute(block, "resp", ring_route(lambda x, c: (x, 1 - c)))
    relay = jnp.where(my_index % 2 == 0, from_plus, from_minus)
    far = lax.ppermute(relay, "resp", ring_route(lambda x, c: (x - 1, c) if c == 0 else (x + 1, c)))
    core_sides = lax.ppermute(
        jnp.concatenate([from_minus, from_plus], 0), "resp", ring_route(lambda x, c: (x, 1 - c))
    )
    far_other = lax.ppermute(far, "resp", ring_route(lambda x, c: (x, 1 - c)))
    return jnp.concatenate(
        [block, from_minus, from_plus, far, from_core, core_sides, far_other], 0
    )


def return_group(terms, my_index):
    def send(block, move):
        return lax.ppermute(block.astype(jnp.bfloat16), "resp", ring_route(move)).astype(jnp.float32)

    kept = terms[:4] + send(terms[4:], lambda x, c: (x, 1 - c))
    own, minus, plus, far = kept[0], kept[1], kept[2], kept[3]
    far_back = send(far, lambda x, c: (x + 1, c) if c == 0 else (x - 1, c))
    is_core0 = my_index % 2 == 0
    plus = plus + jnp.where(is_core0, far_back, 0.0)
    minus = minus + jnp.where(is_core0, 0.0, far_back)
    return own + send(minus, lambda x, c: (x - 1, c)) + send(plus, lambda x, c: (x + 1, c))


def head_sum(row_part):
    heads = lax.axis_size("head")
    quad = row_part
    for distance in range(1, 4):
        quad = quad + lax.ppermute(row_part, "head", [(low, low ^ distance) for low in range(heads)])
    return quad + lax.ppermute(quad, "head", [(low, low ^ 4) for low in range(heads)])


def body(queries, key_states, value_states, partners, counts, norm_gain, out_grad):
    my_index = lax.axis_index("resp")
    seq_len = queries.shape[1]
    count = counts.astype(jnp.int32)
    ring_rows = ring_row(partners[0], my_index)
    group_keys = gather_group(key_states, my_index)
    group_values = gather_group(value_states, my_index)

    attention, log_total = attention_forward(count, ring_rows, queries[0], group_keys, group_values)
    attention_flat = attention.astype(jnp.float32)
    scaled_grad = out_grad[0].astype(jnp.float32) * norm_gain
    row_sums = jnp.stack(
        [jnp.sum(attention_flat * attention_flat, -1), jnp.sum(attention_flat * scaled_grad, -1)]
    )
    row_sums = head_sum(row_sums)
    square_sums, dot_sums = row_sums[0], row_sums[1]
    inverse_rms = lax.rsqrt(square_sums / D + EPSILON)
    normed_out = (attention_flat * inverse_rms[:, None] * norm_gain).astype(jnp.bfloat16)[None]
    attention_grad = (
        inverse_rms[:, None] * scaled_grad
        - attention_flat * (inverse_rms**3 * dot_sums / D)[:, None]
    ).astype(jnp.bfloat16)

    query_grads, key_terms, value_terms = attention_backward(
        count, ring_rows, queries[0], group_keys, group_values, attention_grad, attention, log_total
    )
    zero_rows = jnp.zeros((GROUP,) + key_terms.shape[1:], jnp.float32)
    key_total = return_group(zero_rows.at[ring_rows].add(key_terms), my_index)[None]
    value_total = return_group(zero_rows.at[ring_rows].add(value_terms), my_index)[None]
    return (
        normed_out,
        query_grads[None],
        key_total.astype(jnp.bfloat16),
        value_total.astype(jnp.bfloat16),
    )


def solution(mesh):
    placed = (
        P("resp", None, "head"),
        P("resp", None, "head"),
        P("resp", None, "head"),
        P("resp", None),
        P("resp"),
        P("head"),
        P("resp", None, "head"),
    )
    return jax.shard_map(
        body,
        mesh=mesh,
        in_specs=placed,
        out_specs=(
            P("resp", None, "head"),
            P("resp", None, "head"),
            P("resp", None, "head"),
            P("resp", None, "head"),
        ),
        check_vma=False,
    )
```

```python
import functools

import jax
import jax.numpy as jnp
from jax import lax
from jax.experimental import pallas as pl
from jax.experimental.pallas import tpu as pltpu
from jax.sharding import PartitionSpec as P

HD = 128
D = 8192
GROUP = 8
SLOTS = 3


EPSILON = 1e-05
SCORE_SCALE = HD ** (-0.5)

TRANS_B = (((1,), (1,)), ((), ()))
TRANS_A = (((0,), (0,)), ((), ()))


def slot_scores(query_head, mate_keys):
    scores = lax.dot_general(query_head, mate_keys, TRANS_B, preferred_element_type=jnp.float32)
    return scores * SCORE_SCALE


def slot_offset(count_ref, slot, offset, dead):
    return jnp.where(slot < count_ref[0], offset, dead)


def as_lane_row(column):
    return jnp.transpose(jnp.broadcast_to(column, (column.shape[0], HD)))[:1]


def forward_kernel(count_ref, rows_ref, q_ref, *refs):
    k_ref, v_ref, (out_ref, lse_ref) = refs[:SLOTS], refs[SLOTS : 2 * SLOTS], refs[2 * SLOTS :]
    query_head = q_ref[...]
    scores = [slot_scores(query_head, k_ref[slot][...]) for slot in range(SLOTS)]
    row_max = functools.reduce(
        jnp.maximum,
        [
            slot_offset(count_ref, slot, jnp.max(block, axis=1, keepdims=True), -jnp.inf)
            for slot, block in enumerate(scores)
        ],
    )
    exps = [
        jnp.exp(block - slot_offset(count_ref, slot, row_max, jnp.inf))
        for slot, block in enumerate(scores)
    ]
    denominator = sum(jnp.sum(block, axis=1, keepdims=True) for block in exps)
    weighted = sum(
        jnp.dot(exps[slot].astype(jnp.bfloat16), v_ref[slot][...], preferred_element_type=jnp.float32)
        for slot in range(SLOTS)
    )
    out_ref[...] = (weighted / denominator).astype(out_ref.dtype)
    lse_ref[...] = as_lane_row(row_max + jnp.log(denominator))


def backward_kernel(count_ref, rows_ref, q_ref, *refs):
    k_ref, v_ref = refs[:SLOTS], refs[SLOTS : 2 * SLOTS]
    grad_ref, att_ref, lse_ref, dq_ref, dk_ref, dv_ref = refs[2 * SLOTS :]

    @pl.when(pl.program_id(0) == 0)
    def _():
        dk_ref[...] = jnp.zeros_like(dk_ref)
        dv_ref[...] = jnp.zeros_like(dv_ref)

    query_head = q_ref[...]
    grad_head = grad_ref[...]
    log_total = lse_ref[...]
    row_delta = as_lane_row(
        jnp.sum(grad_head.astype(jnp.float32) * att_ref[...].astype(jnp.float32), axis=1, keepdims=True)
    )
    query_grad = jnp.zeros(dq_ref.shape, jnp.float32)
    for slot in range(SLOTS):
        mate_keys = k_ref[slot][...]
        back_probs = jnp.exp(
            slot_scores(mate_keys, query_head) - slot_offset(count_ref, slot, log_total, jnp.inf)
        )
        dv_ref[slot] += jnp.dot(
            back_probs.astype(jnp.bfloat16), grad_head, preferred_element_type=jnp.float32
        )
        prob_grad = lax.dot_general(
            v_ref[slot][...], grad_head, TRANS_B, preferred_element_type=jnp.float32
        )
        score_grad = (back_probs * (prob_grad - row_delta)).astype(jnp.bfloat16)
        dk_ref[slot] += SCORE_SCALE * jnp.dot(
            score_grad, query_head, preferred_element_type=jnp.float32
        )
        query_grad = query_grad + lax.dot_general(
            score_grad, mate_keys, TRANS_A, preferred_element_type=jnp.float32
        )
    dq_ref[...] = (SCORE_SCALE * query_grad).astype(dq_ref.dtype)


def slot_blocks(seq_len):
    return [
        pl.BlockSpec((None, seq_len, HD), lambda h, c, r, slot=slot: (r[slot], 0, 0))
        for slot in range(SLOTS)
    ]


def attention_forward(count, mate_rows, queries, group_keys, group_values):
    seq_len, width = queries.shape
    heads = width // HD
    head_block = pl.BlockSpec((seq_len, HD), lambda h, c, r: (0, h))
    return pl.pallas_call(
        forward_kernel,
        grid_spec=pltpu.PrefetchScalarGridSpec(
            num_scalar_prefetch=2,
            grid=(heads,),
            in_specs=[head_block] + slot_blocks(seq_len) * 2,
            out_specs=[head_block, pl.BlockSpec((None, 1, seq_len), lambda h, c, r: (h, 0, 0))],
        ),
        out_shape=[
            jax.ShapeDtypeStruct((seq_len, width), jnp.bfloat16),
            jax.ShapeDtypeStruct((heads, 1, seq_len), jnp.float32),
        ],
    )(count, mate_rows, queries, *([group_keys] * SLOTS), *([group_values] * SLOTS))


def attention_backward(
    count, mate_rows, queries, group_keys, group_values, attention_grad, attention, log_rows
):
    seq_len, width = queries.shape
    heads = width // HD
    head_block = pl.BlockSpec((seq_len, HD), lambda h, c, r: (0, h))
    row_block = pl.BlockSpec((None, 1, seq_len), lambda h, c, r: (h, 0, 0))
    slot_block = pl.BlockSpec((SLOTS, seq_len, HD), lambda h, c, r: (0, 0, 0))
    return pl.pallas_call(
        backward_kernel,
        grid_spec=pltpu.PrefetchScalarGridSpec(
            num_scalar_prefetch=2,
            grid=(heads,),
            in_specs=[head_block] + slot_blocks(seq_len) * 2 + [head_block, head_block, row_block],
            out_specs=[head_block, slot_block, slot_block],
        ),
        out_shape=[
            jax.ShapeDtypeStruct((seq_len, width), jnp.bfloat16),
            jax.ShapeDtypeStruct((SLOTS, seq_len, HD), jnp.float32),
            jax.ShapeDtypeStruct((SLOTS, seq_len, HD), jnp.float32),
        ],
        compiler_params=pltpu.CompilerParams(dimension_semantics=("arbitrary",)),
    )(
        count, mate_rows, queries, *([group_keys] * SLOTS), *([group_values] * SLOTS),
        attention_grad, attention, log_rows,
    )


def exchange(block, axis, bit):
    route = [(low, low ^ (1 << bit)) for low in range(lax.axis_size(axis))]
    return lax.ppermute(block, axis, route)


def ring_route(move):
    route = []
    for low in range(lax.axis_size("resp")):
        place = low % GROUP
        chip, core = divmod(place, 2)
        to_chip, to_core = move(chip, core)
        route.append((low, low - place + (to_chip % (GROUP // 2)) * 2 + to_core))
    return route


def ring_row(partner, my_index):
    chip_step = ((partner >> 1) - (my_index >> 1)) % (GROUP // 2)
    other_core = (partner ^ my_index) & 1
    step_row = jnp.where(chip_step == 1, 2, jnp.where(chip_step == 2, 3, jnp.where(chip_step == 3, 1, 0)))
    return other_core * 4 + step_row


def gather_group(block, my_index):
    from_minus = lax.ppermute(block, "resp", ring_route(lambda x, c: (x + 1, c)))
    from_plus = lax.ppermute(block, "resp", ring_route(lambda x, c: (x - 1, c)))
    relay = jnp.where(my_index % 2 == 0, from_plus, from_minus)
    far = lax.ppermute(relay, "resp", ring_route(lambda x, c: (x - 1, c) if c == 0 else (x + 1, c)))
    mine = jnp.concatenate([block, from_minus, from_plus, far], 0)
    other = lax.ppermute(mine, "resp", ring_route(lambda x, c: (x, 1 - c)))
    return jnp.concatenate([mine, other], 0)


def return_group(terms, my_index):
    def send(block, move):
        return lax.ppermute(block.astype(jnp.bfloat16), "resp", ring_route(move)).astype(jnp.float32)

    kept = terms[:4] + send(terms[4:], lambda x, c: (x, 1 - c))
    own, minus, plus, far = kept[0], kept[1], kept[2], kept[3]
    far_back = send(far, lambda x, c: (x + 1, c) if c == 0 else (x - 1, c))
    is_core0 = my_index % 2 == 0
    plus = plus + jnp.where(is_core0, far_back, 0.0)
    minus = minus + jnp.where(is_core0, 0.0, far_back)
    return own + send(minus, lambda x, c: (x - 1, c)) + send(plus, lambda x, c: (x + 1, c))


def head_sum(row_part):
    heads = lax.axis_size("head")
    quad = row_part
    for distance in range(1, 4):
        quad = quad + lax.ppermute(row_part, "head", [(low, low ^ distance) for low in range(heads)])
    return quad + lax.ppermute(quad, "head", [(low, low ^ 4) for low in range(heads)])


def body(queries, key_states, value_states, partners, counts, norm_gain, out_grad):
    my_index = lax.axis_index("resp")
    seq_len = queries.shape[1]
    count = counts.astype(jnp.int32)
    ring_rows = ring_row(partners[0], my_index)
    group_keys = gather_group(key_states, my_index)
    group_values = gather_group(value_states, my_index)

    attention, log_total = attention_forward(count, ring_rows, queries[0], group_keys, group_values)
    attention_flat = attention.astype(jnp.float32)
    scaled_grad = out_grad[0].astype(jnp.float32) * norm_gain
    row_sums = jnp.stack(
        [jnp.sum(attention_flat * attention_flat, -1), jnp.sum(attention_flat * scaled_grad, -1)]
    )
    row_sums = head_sum(row_sums)
    square_sums, dot_sums = row_sums[0], row_sums[1]
    inverse_rms = lax.rsqrt(square_sums / D + EPSILON)
    normed_out = (attention_flat * inverse_rms[:, None] * norm_gain).astype(jnp.bfloat16)[None]
    attention_grad = (
        inverse_rms[:, None] * scaled_grad
        - attention_flat * (inverse_rms**3 * dot_sums / D)[:, None]
    ).astype(jnp.bfloat16)

    query_grads, key_terms, value_terms = attention_backward(
        count, ring_rows, queries[0], group_keys, group_values, attention_grad, attention, log_total
    )
    zero_rows = jnp.zeros((GROUP,) + key_terms.shape[1:], jnp.float32)
    key_total = return_group(zero_rows.at[ring_rows].add(key_terms), my_index)[None]
    value_total = return_group(zero_rows.at[ring_rows].add(value_terms), my_index)[None]
    return (
        normed_out,
        query_grads[None],
        key_total.astype(jnp.bfloat16),
        value_total.astype(jnp.bfloat16),
    )


def solution(mesh):
    placed = (
        P("resp", None, "head"),
        P("resp", None, "head"),
        P("resp", None, "head"),
        P("resp", None),
        P("resp"),
        P("head"),
        P("resp", None, "head"),
    )
    return jax.shard_map(
        body,
        mesh=mesh,
        in_specs=placed,
        out_specs=(
            P("resp", None, "head"),
            P("resp", None, "head"),
            P("resp", None, "head"),
            P("resp", None, "head"),
        ),
        check_vma=False,
    )
```
